512 devices in a mesh: req: 64 (over z, x_hi, core), tp: 8 (over x_lo, y).
Axes of the slice: x: 4 (x_hi: 2, x_lo: 2; x = x_hi * 2 + x_lo), y: 4, z: 16, core: 2. Of those that a mesh axis runs over, the one named last changes fastest.
Arguments:
- query: bfloat16 [7168, 3072], P('req', 'tp'), may hold values from -48 to 48
- key: bfloat16 [7168, 3072], P('req', 'tp'), may hold values from -12 to 12
- value: bfloat16 [7168, 3072], P('req', 'tp'), may hold values from -6 to 6
- cross_query: bfloat16 [7168, 3072], P('req', 'tp'), may hold values from -48 to 48
- text_key: bfloat16 [2048, 3072], P('req', 'tp'), may hold values from -12 to 12
- text_value: bfloat16 [2048, 3072], P('req', 'tp'), may hold values from -6 to 6
- wo_self: bfloat16 [3072, 5120], P('tp', 'req'), may hold values from -3 to 3
- wo_cross: bfloat16 [3072, 5120], P('tp', 'req'), may hold values from -3 to 3
- attn_gate: float32 [4, 5120], replicated, may hold values from 0.5 to 1.5
- mix_coef: float32 [5120], P('tp'), may hold values from 0.1 to 0.4
- latent: bfloat16 [7168, 5120], P('req', 'tp'), may hold values from -6 to 6
- tenant_len: int32 [4], replicated, may hold values from 1 to 1792, as said below
- text_len: int32 [4], replicated, may hold values from 2 to 512, as said below
- t_index: int32 [4], replicated, may hold values from 0 to 49
Outputs:
- velocity: bfloat16 [7168, 5120], P('req', 'tp')
- updated: float32 [7168, 5120], P('req', 'tp')
The draws below stay inside these ranges and needn't reach their ends.
Inputs may be any that keep to these rules, and one draw needn't show every extreme that they name: `tenant_len`: tenant t's latent tokens fill the slots of req indices t, t + 4, t + 8, ... in order from the first slot; one tenant fills all 1792 slots. `text_len`: one tenant's prompt has all 512 tokens.
All inputs are finite; a program needn't handle non-finite values.
Results may differ from the reference program's by a relative error of at most 0.019.
Values may be sent and summed in bfloat16 or wider, within the bound.
No kernel may reach another device: no remote copies, remote signals or barrier semaphores. Data moves between devices by JAX's collectives and lax.ppermute only.
A program may use at most 64 MiB of HBM per device.

```python
import math
import jax
import jax.numpy as jnp
from jax import lax

D = 5120
HEADS = 24
DH = 128
TEXT = 512
TENANTS = 4
STEPS = 50
TILE = 112
GROUP = 16
TOKENS = 7168
N_REQ = 64
N_TP = 8


def latent_pair(key):
    width = HEADS * DH
    keys = jax.random.truncated_normal(jax.random.fold_in(key, 11), -6.0, 6.0, (TOKENS, width), jnp.float32)
    queries = jax.random.truncated_normal(jax.random.fold_in(key, 12), -6.0, 6.0, (TOKENS, width), jnp.float32)
    return (queries, keys)


def text_pair(key):
    width = HEADS * DH
    rows_all = TENANTS * TEXT
    tkeys = jax.random.truncated_normal(jax.random.fold_in(key, 21), -6.0, 6.0, (rows_all, width), jnp.float32)
    queries = jax.random.truncated_normal(jax.random.fold_in(key, 22), -6.0, 6.0, (TOKENS, width), jnp.float32)
    return (queries, tkeys)


def draw_query(key, part):
    return latent_pair(key)[0].astype(jnp.bfloat16)


def draw_key(key, part):
    return latent_pair(key)[1].astype(jnp.bfloat16)


def draw_cross_query(key, part):
    return text_pair(key)[0].astype(jnp.bfloat16)


def draw_text_key(key, part):
    return text_pair(key)[1].astype(jnp.bfloat16)


def draw_tenant_len(key, part):
    full = GROUP * TILE
    quarter = full // TENANTS
    order = jax.random.permutation(jax.random.fold_in(key, 31), TENANTS)
    jitter = jax.random.randint(jax.random.fold_in(key, 32), (TENANTS,), 0, TILE // 2 + 1)
    small = jax.random.randint(jax.random.fold_in(key, 33), (TENANTS,), 1, quarter + 1)
    base = full * (TENANTS - order) // TENANTS - jitter
    base = jnp.where(order == TENANTS - 1, small, base)
    return jnp.where(order == 0, full, jnp.maximum(base, 1)).astype(jnp.int32)


def draw_text_len(key, part):
    lens = jax.random.randint(jax.random.fold_in(key, 41), (TENANTS,), 2, TEXT + 1)
    which = jax.random.randint(jax.random.fold_in(key, 42), (), 0, TENANTS)
    return jnp.where(jnp.arange(TENANTS) == which, TEXT, lens).astype(jnp.int32)


def plant(values, rng, least, high):
    index_at = [jax.random.randint(jax.random.fold_in(rng, axis), (), 0, length) for axis, length in enumerate(values.shape)]
    main_axis = values.shape.index(max(values.shape))
    next_to = index_at[:main_axis] + [(index_at[main_axis] + 1) % values.shape[main_axis]] + index_at[main_axis + 1:]
    return values.at[tuple(index_at)].set(least).at[tuple(next_to)].set(high)


def levels(key, dims, shards, low, top_value):
    loudness, own = 1.0, jax.random.fold_in(key, 6)
    for position, shards_of in shards:
        heights = jnp.exp(jax.random.uniform(jax.random.fold_in(own, position), (shards_of,), jnp.float32, low / len(shards), top_value / len(shards)))
        loudness = loudness * jnp.repeat(heights, dims[position] // shards_of).reshape([-1 if axis == position else 1 for axis in range(len(dims))])
    return loudness


def noise(rng, dims, spread, reach, shards=(), kind=jnp.bfloat16):
    loudness = levels(rng, dims, shards, -0.22, 0.18) if shards else 1.0
    entries = jax.random.normal(rng, dims, jnp.float32) * spread * loudness
    return jnp.minimum(jnp.maximum(entries, -reach), reach).astype(kind)


def setup_inputs(seed: int = 0) -> dict:
    splits = jax.random.split(jax.random.key(seed), 15)
    return {
        "query": draw_query(jax.random.fold_in(splits[14], 71), 0),
        "key": draw_key(jax.random.fold_in(splits[14], 71), 0),
        "value": noise(splits[2], (TOKENS, HEADS * DH), 1.0, 6.0, ((0, 64), (1, 8))),
        "cross_query": draw_cross_query(jax.random.fold_in(splits[14], 71), 0),
        "text_key": draw_text_key(jax.random.fold_in(splits[14], 71), 0),
        "text_value": noise(splits[5], (TENANTS * TEXT, HEADS * DH), 1.0, 6.0, ((0, 64), (1, 8))),
        "wo_self": noise(splits[6], (HEADS * DH, D), 0.5, 3.0, ((0, 8), (1, 64))),
        "wo_cross": noise(splits[7], (HEADS * DH, D), 0.5, 3.0, ((0, 8), (1, 64))),
        "attn_gate": jnp.clip(jax.random.uniform(splits[8], (TENANTS, D), jnp.float32, 0.5, 1.5), 0.5, 1.5),
        "mix_coef": jnp.clip(jnp.exp(math.log(0.4) - 1.3862944 * jax.random.uniform(splits[9], (D,), jnp.float32) ** levels(splits[9], (D,), ((0, 8),), -0.2, 0.2)), 0.1, 0.4),
        "latent": noise(splits[10], (TOKENS, D), 1.0, 6.0, ((0, 64), (1, 8))),
        "tenant_len": draw_tenant_len(jax.random.fold_in(splits[14], 71), 0),
        "text_len": draw_text_len(jax.random.fold_in(splits[14], 71), 0),
        "t_index": plant(jax.random.randint(splits[13], (TENANTS,), 0, STEPS), jax.random.fold_in(splits[13], 1), 0, STEPS - 1).astype(jnp.int32),
    }


def attend(queries, keys, values, valid):
    heads = queries.shape[1] // DH
    q_heads = queries.reshape(queries.shape[0], heads, DH).transpose(1, 0, 2)
    k_heads = keys.reshape(keys.shape[0], heads, DH).transpose(1, 0, 2)
    v_heads = values.reshape(values.shape[0], heads, DH).transpose(1, 0, 2)
    scale = 1.0 / (DH ** 0.5)

    def one_head(items):
        q_one, k_one, v_one = items
        scores = jnp.dot(q_one, k_one.T, preferred_element_type=jnp.float32) * scale
        scores = jnp.where(valid[None, :], scores, -1e30)
        top = jnp.max(scores, axis=-1, keepdims=True)
        weights = jnp.where(valid[None, :], jnp.exp(scores - top), 0.0)
        denom = jnp.sum(weights, axis=-1, keepdims=True)
        mixed = jnp.dot(weights.astype(jnp.bfloat16), v_one, preferred_element_type=jnp.float32)
        return (mixed / denom).astype(jnp.bfloat16)

    out = lax.map(one_head, (q_heads, k_heads, v_heads))
    return out.transpose(1, 0, 2).reshape(queries.shape[0], heads * DH)


def tenant_rows(array, per_dev, tenant):
    group = array.shape[0] // (per_dev * TENANTS)
    return array.reshape(group, TENANTS, per_dev, array.shape[1])[:, tenant].reshape(group * per_dev, array.shape[1])


def reference(query, key, value, cross_query, text_key, text_value, wo_self, wo_cross, attn_gate, mix_coef, latent, tenant_len, text_len, t_index):
    group = N_REQ // TENANTS
    text_dev = TEXT // group
    width = HEADS * DH // N_TP
    vel_list = []
    upd_list = []
    for tenant in range(TENANTS):
        q_t = tenant_rows(query, TILE, tenant)
        k_t = tenant_rows(key, TILE, tenant)
        v_t = tenant_rows(value, TILE, tenant)
        cq_t = tenant_rows(cross_query, TILE, tenant)
        tk_t = tenant_rows(text_key, text_dev, tenant)
        tv_t = tenant_rows(text_value, text_dev, tenant)
        lat_t = tenant_rows(latent, TILE, tenant)
        positions = jnp.arange(group * TILE, dtype=jnp.int32)
        valid = positions < tenant_len[tenant]
        text_valid = jnp.arange(TEXT, dtype=jnp.int32) < text_len[tenant]
        self_out = attend(q_t, k_t, v_t, valid)
        cross_out = attend(cq_t, tk_t, tv_t, text_valid)
        gate = attn_gate[tenant]
        total = jnp.zeros((group * TILE, D), jnp.float32)
        for part in range(N_TP):
            lo = part * width
            s_term = jnp.dot(self_out[:, lo:lo + width], wo_self[lo:lo + width], preferred_element_type=jnp.float32)
            c_term = jnp.dot(cross_out[:, lo:lo + width], wo_cross[lo:lo + width], preferred_element_type=jnp.float32)
            rounded = lax.optimization_barrier((gate[None, :] * s_term + c_term).astype(jnp.bfloat16))
            total = total + rounded.astype(jnp.float32)
        branch = jnp.where(valid[:, None], total.astype(jnp.bfloat16), jnp.zeros((), jnp.bfloat16))
        branch32 = branch.astype(jnp.float32)
        padded = jnp.pad(branch32, ((1, 1), (0, 0)))
        vel = branch32 + mix_coef[None, :] * (padded[:-2] + padded[2:] - 2.0 * branch32)
        vel = jnp.where(valid[:, None], vel, 0.0)
        frac = 1.0 - t_index[tenant].astype(jnp.float32) / STEPS
        sigma = 5.0 * frac / (1.0 + 4.0 * frac)
        upd = lat_t.astype(jnp.float32) + sigma * vel
        vel_list.append(vel.astype(jnp.bfloat16).reshape(group, TILE, D))
        upd_list.append(upd.reshape(group, TILE, D))
    velocity = jnp.stack(vel_list, axis=1).reshape(group * TENANTS * TILE, D)
    updated = jnp.stack(upd_list, axis=1).reshape(group * TENANTS * TILE, D)
    return velocity, updated
```

```python
import jax
import jax.numpy as jnp
from jax import lax
from jax.sharding import Mesh, PartitionSpec as P

DH = 128
TENANTS = 4
STEPS = 50


def attend(q_rows, keys, values, valid):
    rows, feat = q_rows.shape
    heads = feat // DH
    q_heads = q_rows.reshape(rows, heads, DH)
    k_heads = keys.reshape(keys.shape[0], heads, DH)
    v_heads = values.reshape(values.shape[0], heads, DH)
    scores = jnp.einsum("qhd,khd->hqk", q_heads, k_heads, preferred_element_type=jnp.float32) * (
        1.0 / DH**0.5
    )
    scores = jnp.where(valid[None, None, :], scores, -1e30)
    top = jnp.max(scores, axis=-1, keepdims=True)
    weights = jnp.where(valid[None, None, :], jnp.exp(scores - top), 0.0)
    denom = jnp.sum(weights, axis=-1)
    mixed = jnp.einsum(
        "hqk,khd->hqd", weights.astype(jnp.bfloat16), v_heads, preferred_element_type=jnp.float32
    )
    out = mixed / denom[..., None]
    return out.transpose(1, 0, 2).reshape(rows, feat).astype(jnp.bfloat16)


def shards(
    query,
    key,
    value,
    cross_query,
    text_key,
    text_value,
    wo_self,
    wo_cross,
    attn_gate,
    mix_coef,
    latent,
    tenant_len,
    text_len,
    t_index,
):
    tiles, feat = query.shape
    text_rows = text_key.shape[0]
    cols = wo_self.shape[1]
    group = lax.axis_size("z")
    quads = lax.axis_size("q")
    parts = lax.axis_size("tp")
    slot = lax.axis_index("z")
    tenant = lax.axis_index("q")
    picker = jnp.arange(TENANTS) == tenant
    my_len = jnp.sum(jnp.where(picker, tenant_len, 0))
    my_text = jnp.sum(jnp.where(picker, text_len, 0))
    my_step = jnp.sum(jnp.where(picker, t_index, 0))

    packed = jnp.concatenate(
        [key, value, text_key, text_value, query[:1], query[-1:], cross_query[:1], cross_query[-1:]],
        axis=0,
    )
    gathered = lax.all_gather(packed, "z", axis=0, tiled=False)
    at = 0
    keys_all = gathered[:, at : at + tiles].reshape(group * tiles, feat)
    at += tiles
    values_all = gathered[:, at : at + tiles].reshape(group * tiles, feat)
    at += tiles
    tkeys_all = gathered[:, at : at + text_rows].reshape(group * text_rows, feat)
    at += text_rows
    tvalues_all = gathered[:, at : at + text_rows].reshape(group * text_rows, feat)
    at += text_rows
    edges = gathered[:, at : at + 4]
    before = (slot + group - 1) % group
    after = (slot + 1) % group
    prev_edge = lax.dynamic_index_in_dim(edges, before, axis=0, keepdims=False)
    next_edge = lax.dynamic_index_in_dim(edges, after, axis=0, keepdims=False)
    q_rows = jnp.concatenate([query, prev_edge[1:2], next_edge[0:1]], axis=0)
    cq_rows = jnp.concatenate([cross_query, prev_edge[3:4], next_edge[2:3]], axis=0)

    key_valid = jnp.arange(group * tiles, dtype=jnp.int32) < my_len
    text_valid = jnp.arange(group * text_rows, dtype=jnp.int32) < my_text
    self_out = attend(q_rows, keys_all, values_all, key_valid)
    cross_out = attend(cq_rows, tkeys_all, tvalues_all, text_valid)

    w_pair = jnp.stack([wo_self, wo_cross], axis=0)
    w_all = lax.all_gather(w_pair, "z", axis=1, tiled=False)
    w_self = w_all[0].transpose(1, 0, 2).reshape(feat, group * cols)
    w_cross = w_all[1].transpose(1, 0, 2).reshape(feat, group * cols)

    a_pair = jnp.stack([self_out, cross_out], axis=0)
    a_all = lax.all_gather(a_pair, "q", axis=0, tiled=False)
    rows = a_all.shape[2]
    gate = attn_gate.reshape(TENANTS, group, quads, cols)
    gate = lax.dynamic_index_in_dim(gate, tenant, axis=2, keepdims=False).reshape(TENANTS, group * cols)
    s_term = jnp.einsum("qrd,dc->qrc", a_all[:, 0], w_self, preferred_element_type=jnp.float32)
    c_term = jnp.einsum("qrd,dc->qrc", a_all[:, 1], w_cross, preferred_element_type=jnp.float32)
    term = (gate[:, None, :] * s_term + c_term).astype(jnp.bfloat16)
    term = term.reshape(quads, rows, parts, group // parts, cols).transpose(0, 2, 1, 3, 4)
    term = term.reshape(quads * parts, rows, group // parts, cols)
    got = lax.all_to_all(term, ("q", "tp"), 0, 0, tiled=True)
    got = got.reshape(quads, parts, rows, group // parts, cols).astype(jnp.float32)
    total = jnp.sum(got, axis=1)
    total = total.transpose(1, 2, 0, 3).reshape(rows, (group // parts) * quads * cols)
    branch = total.astype(jnp.bfloat16).astype(jnp.float32)

    base = slot * tiles
    row_pos = jnp.concatenate(
        [base + jnp.arange(tiles, dtype=jnp.int32), jnp.stack([base - 1, base + tiles])]
    )
    row_valid = (row_pos >= 0) & (row_pos < my_len) & (row_pos < group * tiles)
    branch = jnp.where(row_valid[:, None], branch, 0.0)
    own = branch[:tiles]
    prev_rows = jnp.concatenate([branch[tiles : tiles + 1], own[:-1]], axis=0)
    next_rows = jnp.concatenate([own[1:], branch[tiles + 1 : tiles + 2]], axis=0)
    vel = own + mix_coef[None, :] * (prev_rows + next_rows - 2.0 * own)
    vel = jnp.where(row_valid[:tiles, None], vel, 0.0)
    frac = 1.0 - my_step.astype(jnp.float32) / STEPS
    sigma = 5.0 * frac / (1.0 + 4.0 * frac)
    updated = latent.astype(jnp.float32) + sigma * vel
    return (vel.astype(jnp.bfloat16), updated)


def solution(mesh):
    req = mesh.shape["req"]
    devices = mesh.devices.reshape(req // TENANTS, TENANTS, mesh.shape["tp"])
    split = Mesh(devices, ("z", "q", "tp"))
    rows = ("z", "q")
    placed = (
        P(rows, "tp"),
        P(rows, "tp"),
        P(rows, "tp"),
        P(rows, "tp"),
        P(rows, "tp"),
        P(rows, "tp"),
        P("tp", rows),
        P("tp", rows),
        P(),
        P("tp"),
        P(rows, "tp"),
        P(),
        P(),
        P(),
    )
    return jax.shard_map(
        shards,
        mesh=split,
        in_specs=placed,
        out_specs=(P(rows, "tp"), P(rows, "tp")),
        check_vma=False,
    )
```

```python
import jax
import jax.numpy as jnp
from jax import lax
from jax.sharding import Mesh, PartitionSpec as P

DH = 128
TENANTS = 4
STEPS = 50


def attend(q_rows, keys, values, valid):
    rows, feat = q_rows.shape
    heads = feat // DH
    q_heads = q_rows.reshape(rows, heads, DH)
    k_heads = keys.reshape(keys.shape[0], heads, DH)
    v_heads = values.reshape(values.shape[0], heads, DH)
    scores = jnp.einsum("qhd,khd->hqk", q_heads, k_heads, preferred_element_type=jnp.float32) * (
        1.0 / DH**0.5
    )
    scores = jnp.where(valid[None, None, :], scores, -1e30)
    top = jnp.max(scores, axis=-1, keepdims=True)
    weights = jnp.where(valid[None, None, :], jnp.exp(scores - top), 0.0)
    denom = jnp.sum(weights, axis=-1)
    mixed = jnp.einsum(
        "hqk,khd->hqd", weights.astype(jnp.bfloat16), v_heads, preferred_element_type=jnp.float32
    )
    out = mixed / denom[..., None]
    return out.transpose(1, 0, 2).reshape(rows, feat).astype(jnp.bfloat16)


def shards(
    query,
    key,
    value,
    cross_query,
    text_key,
    text_value,
    wo_self,
    wo_cross,
    attn_gate,
    mix_coef,
    latent,
    tenant_len,
    text_len,
    t_index,
):
    tiles, feat = query.shape
    text_rows = text_key.shape[0]
    cols = wo_self.shape[1]
    group = lax.axis_size("z")
    quads = lax.axis_size("q")
    parts = lax.axis_size("tp")
    slot = lax.axis_index("z")
    tenant = lax.axis_index("q")
    picker = jnp.arange(TENANTS) == tenant
    my_len = jnp.sum(jnp.where(picker, tenant_len, 0))
    my_text = jnp.sum(jnp.where(picker, text_len, 0))
    my_step = jnp.sum(jnp.where(picker, t_index, 0))

    packed = jnp.concatenate(
        [
            key,
            value,
            text_key,
            text_value,
            wo_self.T,
            wo_cross.T,
            query[:1],
            query[-1:],
            cross_query[:1],
            cross_query[-1:],
        ],
        axis=0,
    )
    gathered = lax.all_gather(packed, "z", axis=0, tiled=False)
    at = 0
    keys_all = gathered[:, at : at + tiles].reshape(group * tiles, feat)
    at += tiles
    values_all = gathered[:, at : at + tiles].reshape(group * tiles, feat)
    at += tiles
    tkeys_all = gathered[:, at : at + text_rows].reshape(group * text_rows, feat)
    at += text_rows
    tvalues_all = gathered[:, at : at + text_rows].reshape(group * text_rows, feat)
    at += text_rows
    w_self_t = gathered[:, at : at + cols]
    at += cols
    w_cross_t = gathered[:, at : at + cols]
    at += cols
    e_g = gathered[:, at : at + 4]
    before = (slot + group - 1) % group
    after = (slot + 1) % group
    prev_edge = lax.dynamic_index_in_dim(e_g, before, axis=0, keepdims=False)
    next_edge = lax.dynamic_index_in_dim(e_g, after, axis=0, keepdims=False)
    q_rows = jnp.concatenate([query, prev_edge[1:2], next_edge[0:1]], axis=0)
    cq_rows = jnp.concatenate([cross_query, prev_edge[3:4], next_edge[2:3]], axis=0)

    key_valid = jnp.arange(group * tiles, dtype=jnp.int32) < my_len
    text_valid = jnp.arange(group * text_rows, dtype=jnp.int32) < my_text
    self_out = attend(q_rows, keys_all, values_all, key_valid)
    cross_out = attend(cq_rows, tkeys_all, tvalues_all, text_valid)

    w_self = w_self_t.transpose(2, 0, 1).reshape(feat, group * cols)
    w_cross = w_cross_t.transpose(2, 0, 1).reshape(feat, group * cols)

    a_pair = jnp.stack([self_out, cross_out], axis=0)
    a_all = lax.all_gather(a_pair, "q", axis=0, tiled=False)
    rows = a_all.shape[2]
    gate = attn_gate.reshape(TENANTS, group, quads, cols)
    gate = lax.dynamic_index_in_dim(gate, tenant, axis=2, keepdims=False).reshape(TENANTS, group * cols)
    s_term = jnp.einsum("qrd,dc->qrc", a_all[:, 0], w_self, preferred_element_type=jnp.float32)
    c_term = jnp.einsum("qrd,dc->qrc", a_all[:, 1], w_cross, preferred_element_type=jnp.float32)
    term = (gate[:, None, :] * s_term + c_term).astype(jnp.bfloat16)
    term = term.reshape(quads, rows, parts, group // parts, cols).transpose(0, 2, 1, 3, 4)
    term = term.reshape(quads * parts, rows, group // parts, cols)
    got = lax.all_to_all(term, ("q", "tp"), 0, 0, tiled=True)
    got = got.reshape(quads, parts, rows, group // parts, cols).astype(jnp.float32)
    total = jnp.sum(got, axis=1)
    total = total.transpose(1, 2, 0, 3).reshape(rows, (group // parts) * quads * cols)
    branch = total.astype(jnp.bfloat16).astype(jnp.float32)

    base = slot * tiles
    row_pos = jnp.concatenate(
        [base + jnp.arange(tiles, dtype=jnp.int32), jnp.stack([base - 1, base + tiles])]
    )
    row_valid = (row_pos >= 0) & (row_pos < my_len) & (row_pos < group * tiles)
    branch = jnp.where(row_valid[:, None], branch, 0.0)
    own = branch[:tiles]
    prev_rows = jnp.concatenate([branch[tiles : tiles + 1], own[:-1]], axis=0)
    next_rows = jnp.concatenate([own[1:], branch[tiles + 1 : tiles + 2]], axis=0)
    vel = own + mix_coef[None, :] * (prev_rows + next_rows - 2.0 * own)
    vel = jnp.where(row_valid[:tiles, None], vel, 0.0)
    frac = 1.0 - my_step.astype(jnp.float32) / STEPS
    sigma = 5.0 * frac / (1.0 + 4.0 * frac)
    updated = latent.astype(jnp.float32) + sigma * vel
    return (vel.astype(jnp.bfloat16), updated)


def solution(mesh):
    req = mesh.shape["req"]
    devices = mesh.devices.reshape(req // TENANTS, TENANTS, mesh.shape["tp"])
    split = Mesh(devices, ("z", "q", "tp"))
    rows = ("z", "q")
    placed = (
        P(rows, "tp"),
        P(rows, "tp"),
        P(rows, "tp"),
        P(rows, "tp"),
        P(rows, "tp"),
        P(rows, "tp"),
        P("tp", rows),
        P("tp", rows),
        P(),
        P("tp"),
        P(rows, "tp"),
        P(),
        P(),
        P(),
    )
    return jax.shard_map(
        shards,
        mesh=split,
        in_specs=placed,
        out_specs=(P(rows, "tp"), P(rows, "tp")),
        check_vma=False,
    )
```

```python
import jax
import jax.numpy as jnp
from jax import lax
from jax.sharding import Mesh, PartitionSpec as P

DH = 128
TENANTS = 4
STEPS = 50


def attend(q_rows, keys, values, valid):
    rows, feat = q_rows.shape
    heads = feat // DH
    q_heads = q_rows.reshape(rows, heads, DH)
    k_heads = keys.reshape(keys.shape[0], heads, DH)
    v_heads = values.reshape(values.shape[0], heads, DH)
    scores = jnp.einsum("qhd,khd->hqk", q_heads, k_heads, preferred_element_type=jnp.float32) * (
        1.0 / DH**0.5
    )
    scores = jnp.where(valid[None, None, :], scores, -1e30)
    top = jnp.max(scores, axis=-1, keepdims=True)
    weights = jnp.where(valid[None, None, :], jnp.exp(scores - top), 0.0)
    denom = jnp.sum(weights, axis=-1)
    mixed = jnp.einsum(
        "hqk,khd->hqd", weights.astype(jnp.bfloat16), v_heads, preferred_element_type=jnp.float32
    )
    out = mixed / denom[..., None]
    return out.transpose(1, 0, 2).reshape(rows, feat).astype(jnp.bfloat16)


def shards(
    query,
    key,
    value,
    cross_query,
    text_key,
    text_value,
    wo_self,
    wo_cross,
    attn_gate,
    mix_coef,
    latent,
    tenant_len,
    text_len,
    t_index,
):
    tiles, feat = query.shape
    text_rows = text_key.shape[0]
    cols = wo_self.shape[1]
    group = lax.axis_size("z")
    quads = lax.axis_size("q")
    parts = lax.axis_size("tp")
    slot = lax.axis_index("z")
    tenant = lax.axis_index("q")
    picker = jnp.arange(TENANTS) == tenant
    my_len = jnp.sum(jnp.where(picker, tenant_len, 0))
    my_text = jnp.sum(jnp.where(picker, text_len, 0))
    my_step = jnp.sum(jnp.where(picker, t_index, 0))

    edges = jnp.concatenate([query[:1], query[-1:], cross_query[:1], cross_query[-1:]], axis=0)
    edges = jnp.pad(edges, ((0, 12), (0, 0)))
    packed = jnp.concatenate(
        [
            key,
            value,
            text_key,
            text_value,
            wo_self.T,
            wo_cross.T,
            edges,
        ],
        axis=0,
    )
    gathered = lax.all_gather(packed, "z", axis=0, tiled=False)
    at = 0
    keys_all = gathered[:, at : at + tiles].reshape(group * tiles, feat)
    at += tiles
    values_all = gathered[:, at : at + tiles].reshape(group * tiles, feat)
    at += tiles
    tkeys_all = gathered[:, at : at + text_rows].reshape(group * text_rows, feat)
    at += text_rows
    tvalues_all = gathered[:, at : at + text_rows].reshape(group * text_rows, feat)
    at += text_rows
    w_self_t = gathered[:, at : at + cols]
    at += cols
    w_cross_t = gathered[:, at : at + cols]
    at += cols
    e_g = gathered[:, at : at + 4]
    before = (slot + group - 1) % group
    after = (slot + 1) % group
    prev_edge = lax.dynamic_index_in_dim(e_g, before, axis=0, keepdims=False)
    next_edge = lax.dynamic_index_in_dim(e_g, after, axis=0, keepdims=False)
    q_rows = jnp.concatenate([query, prev_edge[1:2], next_edge[0:1]], axis=0)
    cq_rows = jnp.concatenate([cross_query, prev_edge[3:4], next_edge[2:3]], axis=0)

    key_valid = jnp.arange(group * tiles, dtype=jnp.int32) < my_len
    text_valid = jnp.arange(group * text_rows, dtype=jnp.int32) < my_text
    self_out = attend(q_rows, keys_all, values_all, key_valid)
    cross_out = attend(cq_rows, tkeys_all, tvalues_all, text_valid)

    w_self = w_self_t.transpose(2, 0, 1).reshape(feat, group * cols)
    w_cross = w_cross_t.transpose(2, 0, 1).reshape(feat, group * cols)

    a_pair = jnp.stack([self_out, cross_out], axis=0)
    a_all = lax.all_gather(a_pair, "q", axis=0, tiled=False)
    rows = a_all.shape[2]
    gate = attn_gate.reshape(TENANTS, group, quads, cols)
    gate = lax.dynamic_index_in_dim(gate, tenant, axis=2, keepdims=False).reshape(TENANTS, group * cols)
    s_term = jnp.einsum("qrd,dc->qrc", a_all[:, 0], w_self, preferred_element_type=jnp.float32)
    c_term = jnp.einsum("qrd,dc->qrc", a_all[:, 1], w_cross, preferred_element_type=jnp.float32)
    term = (gate[:, None, :] * s_term + c_term).astype(jnp.bfloat16)
    term = term.reshape(quads, rows, parts, group // parts, cols).transpose(0, 2, 1, 3, 4)
    term = term.reshape(quads * parts, rows, group // parts, cols)
    got = lax.all_to_all(term, ("q", "tp"), 0, 0, tiled=True)
    got = got.reshape(quads, parts, rows, group // parts, cols).astype(jnp.float32)
    total = jnp.sum(got, axis=1)
    total = total.transpose(1, 2, 0, 3).reshape(rows, (group // parts) * quads * cols)
    branch = total.astype(jnp.bfloat16).astype(jnp.float32)

    base = slot * tiles
    row_pos = jnp.concatenate(
        [base + jnp.arange(tiles, dtype=jnp.int32), jnp.stack([base - 1, base + tiles])]
    )
    row_valid = (row_pos >= 0) & (row_pos < my_len) & (row_pos < group * tiles)
    branch = jnp.where(row_valid[:, None], branch, 0.0)
    own = branch[:tiles]
    prev_rows = jnp.concatenate([branch[tiles : tiles + 1], own[:-1]], axis=0)
    next_rows = jnp.concatenate([own[1:], branch[tiles + 1 : tiles + 2]], axis=0)
    vel = own + mix_coef[None, :] * (prev_rows + next_rows - 2.0 * own)
    vel = jnp.where(row_valid[:tiles, None], vel, 0.0)
    frac = 1.0 - my_step.astype(jnp.float32) / STEPS
    sigma = 5.0 * frac / (1.0 + 4.0 * frac)
    updated = latent.astype(jnp.float32) + sigma * vel
    return (vel.astype(jnp.bfloat16), updated)


def solution(mesh):
    req = mesh.shape["req"]
    devices = mesh.devices.reshape(req // TENANTS, TENANTS, mesh.shape["tp"])
    split = Mesh(devices, ("z", "q", "tp"))
    rows = ("z", "q")
    placed = (
        P(rows, "tp"),
        P(rows, "tp"),
        P(rows, "tp"),
        P(rows, "tp"),
        P(rows, "tp"),
        P(rows, "tp"),
        P("tp", rows),
        P("tp", rows),
        P(),
        P("tp"),
        P(rows, "tp"),
        P(),
        P(),
        P(),
    )
    return jax.shard_map(
        shards,
        mesh=split,
        in_specs=placed,
        out_specs=(P(rows, "tp"), P(rows, "tp")),
        check_vma=False,
    )
```

```python
import jax
import jax.numpy as jnp
from jax import lax
from jax.experimental import pallas as pl
from jax.experimental.pallas import tpu as pltpu
from jax.sharding import Mesh, PartitionSpec as P

DH = 128
TENANTS = 4
STEPS = 50


def attend(q_rows, keys, values, valid):
    rows, feat = q_rows.shape
    heads = feat // DH
    q_heads = q_rows.reshape(rows, heads, DH)
    k_heads = keys.reshape(keys.shape[0], heads, DH)
    v_heads = values.reshape(values.shape[0], heads, DH)
    scores = jnp.einsum("qhd,khd->hqk", q_heads, k_heads, preferred_element_type=jnp.float32) * (
        1.0 / DH**0.5
    )
    scores = jnp.where(valid[None, None, :], scores, -1e30)
    top = jnp.max(scores, axis=-1, keepdims=True)
    weights = jnp.where(valid[None, None, :], jnp.exp(scores - top), 0.0)
    denom = jnp.sum(weights, axis=-1)
    mixed = jnp.einsum(
        "hqk,khd->hqd", weights.astype(jnp.bfloat16), v_heads, preferred_element_type=jnp.float32
    )
    out = mixed / denom[..., None]
    return out.transpose(1, 0, 2).reshape(rows, feat).astype(jnp.bfloat16)


def attention_pair(lens, q_rows, cq_rows, gathered, *, group, tiles, text_rows, stride):
    rows, feat = q_rows.shape
    heads = feat // DH
    scale = 1.0 / DH**0.5
    t_at = 2 * tiles

    def one(q_ref, buf, valid_of, k_off, v_off, width, o_ref):
        for h in range(heads):
            lanes = pl.ds(h * DH, DH)
            q_h = q_ref[:, lanes]

            def scores(j):
                base = j * stride
                k_j = buf[pl.ds(pl.multiple_of(base + k_off, 16), width), lanes]
                s = lax.dot_general(q_h, k_j, (((1,), (1,)), ((), ())), preferred_element_type=jnp.float32)
                s = s * scale
                ok = valid_of(j)
                return jnp.where(ok, s, -1e30), ok

            def top_step(j, m):
                s, _ = scores(j)
                return jnp.maximum(m, jnp.max(s, axis=-1, keepdims=True))

            m = lax.fori_loop(0, group, top_step, jnp.full((rows, 1), -1e30, jnp.float32))

            def sum_step(j, carry):
                den, acc = carry
                s, ok = scores(j)
                p = jnp.where(ok, jnp.exp(s - m), 0.0)
                v_j = buf[pl.ds(pl.multiple_of(j * stride + v_off, 16), width), lanes]
                den = den + jnp.sum(p, axis=-1, keepdims=True)
                acc = acc + jnp.dot(p.astype(jnp.bfloat16), v_j, preferred_element_type=jnp.float32)
                return den, acc

            den, acc = lax.fori_loop(
                0, group, sum_step, (jnp.zeros((rows, 1), jnp.float32), jnp.zeros((rows, DH), jnp.float32))
            )
            o_ref[:, lanes] = (acc / den).astype(o_ref.dtype)

    def kernel(lens_ref, q_ref, cq_ref, buf, o_ref, co_ref):
        n_keys = lens_ref[0]
        n_text = lens_ref[1]

        def self_valid(j):
            pos = j * tiles + lax.broadcasted_iota(jnp.int32, (1, tiles), 1)
            return pos < n_keys

        def text_valid(j):
            pos = j * text_rows + lax.broadcasted_iota(jnp.int32, (1, text_rows), 1)
            return pos < n_text

        one(q_ref, buf, self_valid, 0, tiles, tiles, o_ref)
        one(cq_ref, buf, text_valid, t_at, t_at + text_rows, text_rows, co_ref)

    vmem = pltpu.MemorySpace.VMEM
    return pl.pallas_call(
        kernel,
        out_shape=(
            jax.ShapeDtypeStruct((rows, feat), jnp.bfloat16),
            jax.ShapeDtypeStruct((rows, feat), jnp.bfloat16),
        ),
        in_specs=[
            pl.BlockSpec(memory_space=pltpu.MemorySpace.SMEM),
            pl.BlockSpec(memory_space=vmem),
            pl.BlockSpec(memory_space=vmem),
            pl.BlockSpec(memory_space=vmem),
        ],
        out_specs=(pl.BlockSpec(memory_space=vmem), pl.BlockSpec(memory_space=vmem)),
    )(lens, q_rows, cq_rows, gathered)


def shards(
    query,
    key,
    value,
    cross_query,
    text_key,
    text_value,
    wo_self,
    wo_cross,
    attn_gate,
    mix_coef,
    latent,
    tenant_len,
    text_len,
    t_index,
):
    tiles, feat = query.shape
    text_rows = text_key.shape[0]
    cols = wo_self.shape[1]
    group = lax.axis_size("z")
    quads = lax.axis_size("q")
    parts = lax.axis_size("tp")
    slot = lax.axis_index("z")
    tenant = lax.axis_index("q")
    picker = jnp.arange(TENANTS) == tenant
    my_len = jnp.sum(jnp.where(picker, tenant_len, 0))
    my_text = jnp.sum(jnp.where(picker, text_len, 0))
    my_step = jnp.sum(jnp.where(picker, t_index, 0))

    edges = jnp.concatenate([query[:1], query[-1:], cross_query[:1], cross_query[-1:]], axis=0)
    edges = jnp.pad(edges, ((0, 12), (0, 0)))
    packed = jnp.concatenate(
        [
            key,
            value,
            text_key,
            text_value,
            wo_self.T,
            wo_cross.T,
            edges,
        ],
        axis=0,
    )
    gathered = lax.all_gather(packed, "z", axis=0, tiled=False)
    stride = gathered.shape[1]
    at = 2 * tiles + 2 * text_rows
    w_self_t = gathered[:, at : at + cols]
    at += cols
    w_cross_t = gathered[:, at : at + cols]
    at += cols
    e_g = gathered[:, at : at + 4]
    before = (slot + group - 1) % group
    after = (slot + 1) % group
    prev_edge = lax.dynamic_index_in_dim(e_g, before, axis=0, keepdims=False)
    next_edge = lax.dynamic_index_in_dim(e_g, after, axis=0, keepdims=False)
    pad = (-(tiles + 2)) % 16
    q_rows = jnp.concatenate([query, prev_edge[1:2], next_edge[0:1]], axis=0)
    cq_rows = jnp.concatenate([cross_query, prev_edge[3:4], next_edge[2:3]], axis=0)
    q_rows = jnp.pad(q_rows, ((0, pad), (0, 0)))
    cq_rows = jnp.pad(cq_rows, ((0, pad), (0, 0)))
    lens = jnp.stack([my_len, my_text]).astype(jnp.int32)
    self_out, cross_out = attention_pair(
        lens,
        q_rows,
        cq_rows,
        gathered.reshape(group * stride, feat),
        group=group,
        tiles=tiles,
        text_rows=text_rows,
        stride=stride,
    )
    self_out = self_out[: tiles + 2]
    cross_out = cross_out[: tiles + 2]

    w_self = w_self_t.transpose(2, 0, 1).reshape(feat, group * cols)
    w_cross = w_cross_t.transpose(2, 0, 1).reshape(feat, group * cols)

    a_pair = jnp.stack([self_out, cross_out], axis=0)
    a_all = lax.all_gather(a_pair, "q", axis=0, tiled=False)
    rows = a_all.shape[2]
    gate = attn_gate.reshape(TENANTS, group, quads, cols)
    gate = lax.dynamic_index_in_dim(gate, tenant, axis=2, keepdims=False).reshape(TENANTS, group * cols)
    s_term = jnp.einsum("qrd,dc->qrc", a_all[:, 0], w_self, preferred_element_type=jnp.float32)
    c_term = jnp.einsum("qrd,dc->qrc", a_all[:, 1], w_cross, preferred_element_type=jnp.float32)
    term = (gate[:, None, :] * s_term + c_term).astype(jnp.bfloat16)
    term = term.reshape(quads, rows, parts, group // parts, cols).transpose(0, 2, 1, 3, 4)
    term = term.reshape(quads * parts, rows, group // parts, cols)
    got = lax.all_to_all(term, ("q", "tp"), 0, 0, tiled=True)
    got = got.reshape(quads, parts, rows, group // parts, cols).astype(jnp.float32)
    total = jnp.sum(got, axis=1)
    total = total.transpose(1, 2, 0, 3).reshape(rows, (group // parts) * quads * cols)
    branch = total.astype(jnp.bfloat16).astype(jnp.float32)

    base = slot * tiles
    row_pos = jnp.concatenate(
        [base + jnp.arange(tiles, dtype=jnp.int32), jnp.stack([base - 1, base + tiles])]
    )
    row_valid = (row_pos >= 0) & (row_pos < my_len) & (row_pos < group * tiles)
    branch = jnp.where(row_valid[:, None], branch, 0.0)
    own = branch[:tiles]
    prev_rows = jnp.concatenate([branch[tiles : tiles + 1], own[:-1]], axis=0)
    next_rows = jnp.concatenate([own[1:], branch[tiles + 1 : tiles + 2]], axis=0)
    vel = own + mix_coef[None, :] * (prev_rows + next_rows - 2.0 * own)
    vel = jnp.where(row_valid[:tiles, None], vel, 0.0)
    frac = 1.0 - my_step.astype(jnp.float32) / STEPS
    sigma = 5.0 * frac / (1.0 + 4.0 * frac)
    updated = latent.astype(jnp.float32) + sigma * vel
    return (vel.astype(jnp.bfloat16), updated)


def solution(mesh):
    req = mesh.shape["req"]
    devices = mesh.devices.reshape(req // TENANTS, TENANTS, mesh.shape["tp"])
    split = Mesh(devices, ("z", "q", "tp"))
    rows = ("z", "q")
    placed = (
        P(rows, "tp"),
        P(rows, "tp"),
        P(rows, "tp"),
        P(rows, "tp"),
        P(rows, "tp"),
        P(rows, "tp"),
        P("tp", rows),
        P("tp", rows),
        P(),
        P("tp"),
        P(rows, "tp"),
        P(),
        P(),
        P(),
    )
    return jax.shard_map(
        shards,
        mesh=split,
        in_specs=placed,
        out_specs=(P(rows, "tp"), P(rows, "tp")),
        check_vma=False,
    )
```

```python
import jax
import jax.numpy as jnp
from jax import lax
from jax.experimental import pallas as pl
from jax.experimental.pallas import tpu as pltpu
from jax.sharding import Mesh, PartitionSpec as P

DH = 128
TENANTS = 4
STEPS = 50


def attend(q_rows, keys, values, valid):
    rows, feat = q_rows.shape
    heads = feat // DH
    q_heads = q_rows.reshape(rows, heads, DH)
    k_heads = keys.reshape(keys.shape[0], heads, DH)
    v_heads = values.reshape(values.shape[0], heads, DH)
    scores = jnp.einsum("qhd,khd->hqk", q_heads, k_heads, preferred_element_type=jnp.float32) * (
        1.0 / DH**0.5
    )
    scores = jnp.where(valid[None, None, :], scores, -1e30)
    top = jnp.max(scores, axis=-1, keepdims=True)
    weights = jnp.where(valid[None, None, :], jnp.exp(scores - top), 0.0)
    denom = jnp.sum(weights, axis=-1)
    mixed = jnp.einsum(
        "hqk,khd->hqd", weights.astype(jnp.bfloat16), v_heads, preferred_element_type=jnp.float32
    )
    out = mixed / denom[..., None]
    return out.transpose(1, 0, 2).reshape(rows, feat).astype(jnp.bfloat16)


def attention_pair(lens, q_rows, cq_rows, gathered, *, group, tiles, text_rows, stride):
    rows, feat = q_rows.shape
    heads = feat // DH
    scale = 1.0 / DH**0.5
    t_at = 2 * tiles

    def one(q_ref, buf, valid_of, k_off, v_off, width, o_ref):
        oks = [valid_of(j) for j in range(group)]
        for h in range(heads):
            lanes = pl.ds(h * DH, DH)
            q_h = q_ref[:, lanes]
            blocks = []
            for j in range(group):
                k_j = buf[pl.ds(j * stride + k_off, width), lanes]
                s = lax.dot_general(q_h, k_j, (((1,), (1,)), ((), ())), preferred_element_type=jnp.float32)
                blocks.append(jnp.where(oks[j], s * scale, -1e30))
            m = blocks[0].max(axis=-1, keepdims=True)
            for s in blocks[1:]:
                m = jnp.maximum(m, s.max(axis=-1, keepdims=True))
            den = jnp.zeros((rows, 1), jnp.float32)
            acc = jnp.zeros((rows, DH), jnp.float32)
            for j, s in enumerate(blocks):
                p = jnp.where(oks[j], jnp.exp(s - m), 0.0)
                v_j = buf[pl.ds(j * stride + v_off, width), lanes]
                den = den + jnp.sum(p, axis=-1, keepdims=True)
                acc = acc + jnp.dot(p.astype(jnp.bfloat16), v_j, preferred_element_type=jnp.float32)
            o_ref[:, lanes] = (acc / den).astype(o_ref.dtype)

    def kernel(lens_ref, q_ref, cq_ref, buf, o_ref, co_ref):
        n_keys = lens_ref[0]
        n_text = lens_ref[1]

        def self_valid(j):
            pos = j * tiles + lax.broadcasted_iota(jnp.int32, (1, tiles), 1)
            return pos < n_keys

        def text_valid(j):
            pos = j * text_rows + lax.broadcasted_iota(jnp.int32, (1, text_rows), 1)
            return pos < n_text

        one(q_ref, buf, self_valid, 0, tiles, tiles, o_ref)
        one(cq_ref, buf, text_valid, t_at, t_at + text_rows, text_rows, co_ref)

    vmem = pltpu.MemorySpace.VMEM
    return pl.pallas_call(
        kernel,
        out_shape=(
            jax.ShapeDtypeStruct((rows, feat), jnp.bfloat16),
            jax.ShapeDtypeStruct((rows, feat), jnp.bfloat16),
        ),
        in_specs=[
            pl.BlockSpec(memory_space=pltpu.MemorySpace.SMEM),
            pl.BlockSpec(memory_space=vmem),
            pl.BlockSpec(memory_space=vmem),
            pl.BlockSpec(memory_space=vmem),
        ],
        out_specs=(pl.BlockSpec(memory_space=vmem), pl.BlockSpec(memory_space=vmem)),
    )(lens, q_rows, cq_rows, gathered)


def shards(
    query,
    key,
    value,
    cross_query,
    text_key,
    text_value,
    wo_self,
    wo_cross,
    attn_gate,
    mix_coef,
    latent,
    tenant_len,
    text_len,
    t_index,
):
    tiles, feat = query.shape
    text_rows = text_key.shape[0]
    cols = wo_self.shape[1]
    group = lax.axis_size("z")
    quads = lax.axis_size("q")
    parts = lax.axis_size("tp")
    slot = lax.axis_index("z")
    tenant = lax.axis_index("q")
    picker = jnp.arange(TENANTS) == tenant
    my_len = jnp.sum(jnp.where(picker, tenant_len, 0))
    my_text = jnp.sum(jnp.where(picker, text_len, 0))
    my_step = jnp.sum(jnp.where(picker, t_index, 0))

    edges = jnp.concatenate([query[:1], query[-1:], cross_query[:1], cross_query[-1:]], axis=0)
    edges = jnp.pad(edges, ((0, 12), (0, 0)))
    packed = jnp.concatenate(
        [
            key,
            value,
            text_key,
            text_value,
            wo_self.T,
            wo_cross.T,
            edges,
        ],
        axis=0,
    )
    gathered = lax.all_gather(packed, "z", axis=0, tiled=False)
    stride = gathered.shape[1]
    at = 2 * tiles + 2 * text_rows
    w_self_t = gathered[:, at : at + cols]
    at += cols
    w_cross_t = gathered[:, at : at + cols]
    at += cols
    e_g = gathered[:, at : at + 4]
    before = (slot + group - 1) % group
    after = (slot + 1) % group
    prev_edge = lax.dynamic_index_in_dim(e_g, before, axis=0, keepdims=False)
    next_edge = lax.dynamic_index_in_dim(e_g, after, axis=0, keepdims=False)
    pad = (-(tiles + 2)) % 16
    q_rows = jnp.concatenate([query, prev_edge[1:2], next_edge[0:1]], axis=0)
    cq_rows = jnp.concatenate([cross_query, prev_edge[3:4], next_edge[2:3]], axis=0)
    q_rows = jnp.pad(q_rows, ((0, pad), (0, 0)))
    cq_rows = jnp.pad(cq_rows, ((0, pad), (0, 0)))
    lens = jnp.stack([my_len, my_text]).astype(jnp.int32)
    self_out, cross_out = attention_pair(
        lens,
        q_rows,
        cq_rows,
        gathered.reshape(group * stride, feat),
        group=group,
        tiles=tiles,
        text_rows=text_rows,
        stride=stride,
    )
    self_out = self_out[: tiles + 2]
    cross_out = cross_out[: tiles + 2]

    w_self = w_self_t.transpose(2, 0, 1).reshape(feat, group * cols)
    w_cross = w_cross_t.transpose(2, 0, 1).reshape(feat, group * cols)

    a_pair = jnp.stack([self_out, cross_out], axis=0)
    a_all = lax.all_gather(a_pair, "q", axis=0, tiled=False)
    rows = a_all.shape[2]
    gate = attn_gate.reshape(TENANTS, group, quads, cols)
    gate = lax.dynamic_index_in_dim(gate, tenant, axis=2, keepdims=False).reshape(TENANTS, group * cols)
    s_term = jnp.einsum("qrd,dc->qrc", a_all[:, 0], w_self, preferred_element_type=jnp.float32)
    c_term = jnp.einsum("qrd,dc->qrc", a_all[:, 1], w_cross, preferred_element_type=jnp.float32)
    term = (gate[:, None, :] * s_term + c_term).astype(jnp.bfloat16)
    term = term.reshape(quads, rows, parts, group // parts, cols).transpose(0, 2, 1, 3, 4)
    term = term.reshape(quads * parts, rows, group // parts, cols)
    got = lax.all_to_all(term, ("q", "tp"), 0, 0, tiled=True)
    got = got.reshape(quads, parts, rows, group // parts, cols).astype(jnp.float32)
    total = jnp.sum(got, axis=1)
    total = total.transpose(1, 2, 0, 3).reshape(rows, (group // parts) * quads * cols)
    branch = total.astype(jnp.bfloat16).astype(jnp.float32)

    base = slot * tiles
    row_pos = jnp.concatenate(
        [base + jnp.arange(tiles, dtype=jnp.int32), jnp.stack([base - 1, base + tiles])]
    )
    row_valid = (row_pos >= 0) & (row_pos < my_len) & (row_pos < group * tiles)
    branch = jnp.where(row_valid[:, None], branch, 0.0)
    own = branch[:tiles]
    prev_rows = jnp.concatenate([branch[tiles : tiles + 1], own[:-1]], axis=0)
    next_rows = jnp.concatenate([own[1:], branch[tiles + 1 : tiles + 2]], axis=0)
    vel = own + mix_coef[None, :] * (prev_rows + next_rows - 2.0 * own)
    vel = jnp.where(row_valid[:tiles, None], vel, 0.0)
    frac = 1.0 - my_step.astype(jnp.float32) / STEPS
    sigma = 5.0 * frac / (1.0 + 4.0 * frac)
    updated = latent.astype(jnp.float32) + sigma * vel
    return (vel.astype(jnp.bfloat16), updated)


def solution(mesh):
    req = mesh.shape["req"]
    devices = mesh.devices.reshape(req // TENANTS, TENANTS, mesh.shape["tp"])
    split = Mesh(devices, ("z", "q", "tp"))
    rows = ("z", "q")
    placed = (
        P(rows, "tp"),
        P(rows, "tp"),
        P(rows, "tp"),
        P(rows, "tp"),
        P(rows, "tp"),
        P(rows, "tp"),
        P("tp", rows),
        P("tp", rows),
        P(),
        P("tp"),
        P(rows, "tp"),
        P(),
        P(),
        P(),
    )
    return jax.shard_map(
        shards,
        mesh=split,
        in_specs=placed,
        out_specs=(P(rows, "tp"), P(rows, "tp")),
        check_vma=False,
    )
```

```python
import jax
import jax.numpy as jnp
from jax import lax
from jax.experimental import pallas as pl
from jax.experimental.pallas import tpu as pltpu
from jax.sharding import Mesh, PartitionSpec as P

DH = 128
TENANTS = 4
STEPS = 50


def attend(q_rows, keys, values, valid):
    rows, feat = q_rows.shape
    heads = feat // DH
    q_heads = q_rows.reshape(rows, heads, DH)
    k_heads = keys.reshape(keys.shape[0], heads, DH)
    v_heads = values.reshape(values.shape[0], heads, DH)
    scores = jnp.einsum("qhd,khd->hqk", q_heads, k_heads, preferred_element_type=jnp.float32) * (
        1.0 / DH**0.5
    )
    scores = jnp.where(valid[None, None, :], scores, -1e30)
    top = jnp.max(scores, axis=-1, keepdims=True)
    weights = jnp.where(valid[None, None, :], jnp.exp(scores - top), 0.0)
    denom = jnp.sum(weights, axis=-1)
    mixed = jnp.einsum(
        "hqk,khd->hqd", weights.astype(jnp.bfloat16), v_heads, preferred_element_type=jnp.float32
    )
    out = mixed / denom[..., None]
    return out.transpose(1, 0, 2).reshape(rows, feat).astype(jnp.bfloat16)


def attention_pair(lens, q_rows, cq_rows, gathered, *, group, tiles, text_rows, stride):
    rows, feat = q_rows.shape
    heads = feat // DH
    scale = 1.0 / DH**0.5
    t_at = 2 * tiles

    def one(q_ref, buf, valid_of, k_off, v_off, width, o_ref, which):
        oks = [valid_of(j) for j in range(group)]
        for h in range(heads):
            lanes = pl.ds(h * DH, DH)
            q_h = q_ref[:, lanes]
            blocks = []
            for j in range(group):
                k_j = buf[pl.ds(j * stride + k_off, width), lanes]
                s = lax.dot_general(q_h, k_j, (((1,), (1,)), ((), ())), preferred_element_type=jnp.float32)
                blocks.append(jnp.where(oks[j], s * scale, -1e30))
            m = blocks[0].max(axis=-1, keepdims=True)
            for s in blocks[1:]:
                m = jnp.maximum(m, s.max(axis=-1, keepdims=True))
            den = jnp.zeros((rows, 1), jnp.float32)
            acc = jnp.zeros((rows, DH), jnp.float32)
            for j, s in enumerate(blocks):
                p = jnp.where(oks[j], jnp.exp(s - m), 0.0)
                v_j = buf[pl.ds(j * stride + v_off, width), lanes]
                den = den + jnp.sum(p, axis=-1, keepdims=True)
                acc = acc + jnp.dot(p.astype(jnp.bfloat16), v_j, preferred_element_type=jnp.float32)
            o_ref[which, :, lanes] = (acc / den).astype(o_ref.dtype)

    def kernel(lens_ref, q_ref, cq_ref, buf, o_ref):
        n_keys = lens_ref[0]
        n_text = lens_ref[1]

        def self_valid(j):
            pos = j * tiles + lax.broadcasted_iota(jnp.int32, (1, tiles), 1)
            return pos < n_keys

        def text_valid(j):
            pos = j * text_rows + lax.broadcasted_iota(jnp.int32, (1, text_rows), 1)
            return pos < n_text

        one(q_ref, buf, self_valid, 0, tiles, tiles, o_ref, 0)
        one(cq_ref, buf, text_valid, t_at, t_at + text_rows, text_rows, o_ref, 1)

    vmem = pltpu.MemorySpace.VMEM
    return pl.pallas_call(
        kernel,
        out_shape=jax.ShapeDtypeStruct((2, rows, feat), jnp.bfloat16),
        in_specs=[
            pl.BlockSpec(memory_space=pltpu.MemorySpace.SMEM),
            pl.BlockSpec(memory_space=vmem),
            pl.BlockSpec(memory_space=vmem),
            pl.BlockSpec(memory_space=vmem),
        ],
        out_specs=pl.BlockSpec(memory_space=vmem),
    )(lens, q_rows, cq_rows, gathered)

def pack_block(key, value, text_key, text_value, w_self_t, w_cross_t, query, cross_query):
    pieces = (key, value, text_key, text_value, w_self_t, w_cross_t)
    starts = [0]
    for piece in pieces:
        starts.append(starts[-1] + piece.shape[0])
    edge_rows = 16
    feat = key.shape[1]
    last = query.shape[0] - 1

    def kernel(k_ref, v_ref, tk_ref, tv_ref, ws_ref, wc_ref, q_ref, cq_ref, o_ref):
        refs = (k_ref, v_ref, tk_ref, tv_ref, ws_ref, wc_ref)
        for ref, at in zip(refs, starts):
            o_ref[pl.ds(at, ref.shape[0]), :] = ref[...]
        q = q_ref[...].astype(jnp.float32)
        cq = cq_ref[...].astype(jnp.float32)
        row = lax.broadcasted_iota(jnp.int32, (edge_rows, feat), 0)
        edges = jnp.where(row == 0, q[0:1], 0.0)
        edges = jnp.where(row == 1, q[last : last + 1], edges)
        edges = jnp.where(row == 2, cq[0:1], edges)
        edges = jnp.where(row == 3, cq[last : last + 1], edges)
        o_ref[pl.ds(starts[-1], edge_rows), :] = edges.astype(o_ref.dtype)

    vmem = pltpu.MemorySpace.VMEM
    return pl.pallas_call(
        kernel,
        out_shape=jax.ShapeDtypeStruct((starts[-1] + edge_rows, feat), key.dtype),
        in_specs=[pl.BlockSpec(memory_space=vmem)] * 8,
        out_specs=pl.BlockSpec(memory_space=vmem),
    )(key, value, text_key, text_value, w_self_t, w_cross_t, query, cross_query)


def shards(
    query,
    key,
    value,
    cross_query,
    text_key,
    text_value,
    wo_self,
    wo_cross,
    attn_gate,
    mix_coef,
    latent,
    tenant_len,
    text_len,
    t_index,
):
    tiles, feat = query.shape
    text_rows = text_key.shape[0]
    cols = wo_self.shape[1]
    group = lax.axis_size("z")
    quads = lax.axis_size("q")
    parts = lax.axis_size("tp")
    slot = lax.axis_index("z")
    tenant = lax.axis_index("q")
    picker = jnp.arange(TENANTS) == tenant
    my_len = jnp.sum(jnp.where(picker, tenant_len, 0))
    my_text = jnp.sum(jnp.where(picker, text_len, 0))
    my_step = jnp.sum(jnp.where(picker, t_index, 0))

    packed = pack_block(key, value, text_key, text_value, wo_self.T, wo_cross.T, query, cross_query)
    gathered = lax.all_gather(packed, "z", axis=0, tiled=False)
    stride = gathered.shape[1]
    at = 2 * tiles + 2 * text_rows
    w_self_t = gathered[:, at : at + cols]
    at += cols
    w_cross_t = gathered[:, at : at + cols]
    at += cols
    e_g = gathered[:, at : at + 4]
    before = (slot + group - 1) % group
    after = (slot + 1) % group
    prev_edge = lax.dynamic_index_in_dim(e_g, before, axis=0, keepdims=False)
    next_edge = lax.dynamic_index_in_dim(e_g, after, axis=0, keepdims=False)
    pad = (-(tiles + 2)) % 16
    q_rows = jnp.concatenate([query, prev_edge[1:2], next_edge[0:1]], axis=0)
    cq_rows = jnp.concatenate([cross_query, prev_edge[3:4], next_edge[2:3]], axis=0)
    q_rows = jnp.pad(q_rows, ((0, pad), (0, 0)))
    cq_rows = jnp.pad(cq_rows, ((0, pad), (0, 0)))
    lens = jnp.stack([my_len, my_text]).astype(jnp.int32)
    a_pair = attention_pair(
        lens,
        q_rows,
        cq_rows,
        gathered.reshape(group * stride, feat),
        group=group,
        tiles=tiles,
        text_rows=text_rows,
        stride=stride,
    )

    w_self = w_self_t.transpose(2, 0, 1).reshape(feat, group * cols)
    w_cross = w_cross_t.transpose(2, 0, 1).reshape(feat, group * cols)

    a_all = lax.all_gather(a_pair, "q", axis=0, tiled=False)[:, :, : tiles + 2]
    rows = tiles + 2
    gate = attn_gate.reshape(TENANTS, group, quads, cols)
    gate = lax.dynamic_index_in_dim(gate, tenant, axis=2, keepdims=False).reshape(TENANTS, group * cols)
    s_term = jnp.einsum("qrd,dc->qrc", a_all[:, 0], w_self, preferred_element_type=jnp.float32)
    c_term = jnp.einsum("qrd,dc->qrc", a_all[:, 1], w_cross, preferred_element_type=jnp.float32)
    term = (gate[:, None, :] * s_term + c_term).astype(jnp.bfloat16)
    term = term.reshape(quads, rows, parts, group // parts, cols).transpose(0, 2, 1, 3, 4)
    term = term.reshape(quads * parts, rows, group // parts, cols)
    got = lax.all_to_all(term, ("q", "tp"), 0, 0, tiled=True)
    got = got.reshape(quads, parts, rows, group // parts, cols).astype(jnp.float32)
    total = jnp.sum(got, axis=1)
    total = total.transpose(1, 2, 0, 3).reshape(rows, (group // parts) * quads * cols)
    branch = total.astype(jnp.bfloat16).astype(jnp.float32)

    base = slot * tiles
    row_pos = jnp.concatenate(
        [base + jnp.arange(tiles, dtype=jnp.int32), jnp.stack([base - 1, base + tiles])]
    )
    row_valid = (row_pos >= 0) & (row_pos < my_len) & (row_pos < group * tiles)
    branch = jnp.where(row_valid[:, None], branch, 0.0)
    own = branch[:tiles]
    prev_rows = jnp.concatenate([branch[tiles : tiles + 1], own[:-1]], axis=0)
    next_rows = jnp.concatenate([own[1:], branch[tiles + 1 : tiles + 2]], axis=0)
    vel = own + mix_coef[None, :] * (prev_rows + next_rows - 2.0 * own)
    vel = jnp.where(row_valid[:tiles, None], vel, 0.0)
    frac = 1.0 - my_step.astype(jnp.float32) / STEPS
    sigma = 5.0 * frac / (1.0 + 4.0 * frac)
    updated = latent.astype(jnp.float32) + sigma * vel
    return (vel.astype(jnp.bfloat16), updated)


def solution(mesh):
    req = mesh.shape["req"]
    devices = mesh.devices.reshape(req // TENANTS, TENANTS, mesh.shape["tp"])
    split = Mesh(devices, ("z", "q", "tp"))
    rows = ("z", "q")
    placed = (
        P(rows, "tp"),
        P(rows, "tp"),
        P(rows, "tp"),
        P(rows, "tp"),
        P(rows, "tp"),
        P(rows, "tp"),
        P("tp", rows),
        P("tp", rows),
        P(),
        P("tp"),
        P(rows, "tp"),
        P(),
        P(),
        P(),
    )
    return jax.shard_map(
        shards,
        mesh=split,
        in_specs=placed,
        out_specs=(P(rows, "tp"), P(rows, "tp")),
        check_vma=False,
    )
```

```python
import jax
import jax.numpy as jnp
from jax import lax
from jax.experimental import pallas as pl
from jax.experimental.pallas import tpu as pltpu
from jax.sharding import Mesh, PartitionSpec as P

DH = 128
TENANTS = 4
STEPS = 50


def attend(q_rows, keys, values, valid):
    rows, feat = q_rows.shape
    heads = feat // DH
    q_heads = q_rows.reshape(rows, heads, DH)
    k_heads = keys.reshape(keys.shape[0], heads, DH)
    v_heads = values.reshape(values.shape[0], heads, DH)
    scores = jnp.einsum("qhd,khd->hqk", q_heads, k_heads, preferred_element_type=jnp.float32) * (
        1.0 / DH**0.5
    )
    scores = jnp.where(valid[None, None, :], scores, -1e30)
    top = jnp.max(scores, axis=-1, keepdims=True)
    weights = jnp.where(valid[None, None, :], jnp.exp(scores - top), 0.0)
    denom = jnp.sum(weights, axis=-1)
    mixed = jnp.einsum(
        "hqk,khd->hqd", weights.astype(jnp.bfloat16), v_heads, preferred_element_type=jnp.float32
    )
    out = mixed / denom[..., None]
    return out.transpose(1, 0, 2).reshape(rows, feat).astype(jnp.bfloat16)


def attention_pair(lens, q_rows, cq_rows, gathered, *, group, tiles, text_rows, stride):
    rows, feat = q_rows.shape
    heads = feat // DH
    scale = 1.0 / DH**0.5
    t_at = 2 * tiles

    def one(q_ref, buf, valid_of, k_off, v_off, width, o_ref, which):
        oks = [valid_of(j) for j in range(group)]
        for h in range(heads):
            lanes = pl.ds(h * DH, DH)
            q_h = q_ref[:, lanes]
            blocks = []
            for j in range(group):
                k_j = buf[pl.ds(j * stride + k_off, width), lanes]
                s = lax.dot_general(q_h, k_j, (((1,), (1,)), ((), ())), preferred_element_type=jnp.float32)
                blocks.append(jnp.where(oks[j], s * scale, -1e30))
            m = blocks[0].max(axis=-1, keepdims=True)
            for s in blocks[1:]:
                m = jnp.maximum(m, s.max(axis=-1, keepdims=True))
            den = jnp.zeros((rows, 1), jnp.float32)
            acc = jnp.zeros((rows, DH), jnp.float32)
            for j, s in enumerate(blocks):
                p = jnp.where(oks[j], jnp.exp(s - m), 0.0)
                v_j = buf[pl.ds(j * stride + v_off, width), lanes]
                den = den + jnp.sum(p, axis=-1, keepdims=True)
                acc = acc + jnp.dot(p.astype(jnp.bfloat16), v_j, preferred_element_type=jnp.float32)
            o_ref[which, :, lanes] = (acc / den).astype(o_ref.dtype)

    def kernel(lens_ref, q_ref, cq_ref, buf, o_ref):
        n_keys = lens_ref[0]
        n_text = lens_ref[1]

        def self_valid(j):
            pos = j * tiles + lax.broadcasted_iota(jnp.int32, (1, tiles), 1)
            return pos < n_keys

        def text_valid(j):
            pos = j * text_rows + lax.broadcasted_iota(jnp.int32, (1, text_rows), 1)
            return pos < n_text

        one(q_ref, buf, self_valid, 0, tiles, tiles, o_ref, 0)
        one(cq_ref, buf, text_valid, t_at, t_at + text_rows, text_rows, o_ref, 1)

    vmem = pltpu.MemorySpace.VMEM
    return pl.pallas_call(
        kernel,
        out_shape=jax.ShapeDtypeStruct((2, rows, feat), jnp.bfloat16),
        in_specs=[
            pl.BlockSpec(memory_space=pltpu.MemorySpace.SMEM),
            pl.BlockSpec(memory_space=vmem),
            pl.BlockSpec(memory_space=vmem),
            pl.BlockSpec(memory_space=vmem),
        ],
        out_specs=pl.BlockSpec(memory_space=vmem),
    )(lens, q_rows, cq_rows, gathered)

def pack_block(key, value, text_key, text_value, w_self_t, w_cross_t, query, cross_query):
    pieces = (key, value, text_key, text_value, w_self_t, w_cross_t)
    starts = [0]
    for piece in pieces:
        starts.append(starts[-1] + piece.shape[0])
    edge_rows = 16
    feat = key.shape[1]
    last = query.shape[0] - 1

    def kernel(k_ref, v_ref, tk_ref, tv_ref, ws_ref, wc_ref, q_ref, cq_ref, o_ref):
        refs = (k_ref, v_ref, tk_ref, tv_ref, ws_ref, wc_ref)
        for ref, at in zip(refs, starts):
            o_ref[pl.ds(at, ref.shape[0]), :] = ref[...]
        q = q_ref[...].astype(jnp.float32)
        cq = cq_ref[...].astype(jnp.float32)
        row = lax.broadcasted_iota(jnp.int32, (edge_rows, feat), 0)
        edges = jnp.where(row == 0, q[0:1], 0.0)
        edges = jnp.where(row == 1, q[last : last + 1], edges)
        edges = jnp.where(row == 2, cq[0:1], edges)
        edges = jnp.where(row == 3, cq[last : last + 1], edges)
        o_ref[pl.ds(starts[-1], edge_rows), :] = edges.astype(o_ref.dtype)

    vmem = pltpu.MemorySpace.VMEM
    return pl.pallas_call(
        kernel,
        out_shape=jax.ShapeDtypeStruct((starts[-1] + edge_rows, feat), key.dtype),
        in_specs=[pl.BlockSpec(memory_space=vmem)] * 8,
        out_specs=pl.BlockSpec(memory_space=vmem),
    )(key, value, text_key, text_value, w_self_t, w_cross_t, query, cross_query)


def shards(
    query,
    key,
    value,
    cross_query,
    text_key,
    text_value,
    wo_self,
    wo_cross,
    attn_gate,
    mix_coef,
    latent,
    tenant_len,
    text_len,
    t_index,
):
    tiles, feat = query.shape
    text_rows = text_key.shape[0]
    cols = wo_self.shape[1]
    group = lax.axis_size("z")
    quads = lax.axis_size("q")
    parts = lax.axis_size("tp")
    slot = lax.axis_index("z")
    tenant = lax.axis_index("q")
    picker = jnp.arange(TENANTS) == tenant
    my_len = jnp.sum(jnp.where(picker, tenant_len, 0))
    my_text = jnp.sum(jnp.where(picker, text_len, 0))
    my_step = jnp.sum(jnp.where(picker, t_index, 0))

    packed = pack_block(key, value, text_key, text_value, wo_self.T, wo_cross.T, query, cross_query)
    gathered = lax.all_gather(packed, "z", axis=0, tiled=False)
    stride = gathered.shape[1]
    at = 2 * tiles + 2 * text_rows
    w_self_t = gathered[:, at : at + cols]
    at += cols
    w_cross_t = gathered[:, at : at + cols]
    at += cols
    flat = gathered.reshape(group * stride, feat)
    before = (slot + group - 1) % group * stride + at
    after = (slot + 1) % group * stride + at

    def edge(row):
        return lax.dynamic_slice_in_dim(flat, row, 1, axis=0)

    pad = (-(tiles + 2)) % 16
    q_rows = jnp.concatenate([query, edge(before + 1), edge(after)], axis=0)
    cq_rows = jnp.concatenate([cross_query, edge(before + 3), edge(after + 2)], axis=0)
    q_rows = jnp.pad(q_rows, ((0, pad), (0, 0)))
    cq_rows = jnp.pad(cq_rows, ((0, pad), (0, 0)))
    lens = jnp.stack([my_len, my_text]).astype(jnp.int32)
    a_pair = attention_pair(
        lens,
        q_rows,
        cq_rows,
        flat,
        group=group,
        tiles=tiles,
        text_rows=text_rows,
        stride=stride,
    )

    a_all = lax.all_gather(a_pair, "q", axis=0, tiled=False)[:, :, : tiles + 2]
    rows = tiles + 2
    gate = attn_gate.reshape(TENANTS, group, quads, cols)
    gate = lax.dynamic_index_in_dim(gate, tenant, axis=2, keepdims=False).reshape(TENANTS, group * cols)
    s_term = jnp.einsum("qrd,kcd->qrkc", a_all[:, 0], w_self_t, preferred_element_type=jnp.float32)
    c_term = jnp.einsum("qrd,kcd->qrkc", a_all[:, 1], w_cross_t, preferred_element_type=jnp.float32)
    s_term = s_term.reshape(quads, rows, group * cols)
    c_term = c_term.reshape(quads, rows, group * cols)
    term = (gate[:, None, :] * s_term + c_term).astype(jnp.bfloat16)
    term = term.reshape(quads, rows, parts, group // parts, cols).transpose(0, 2, 1, 3, 4)
    term = term.reshape(quads * parts, rows, group // parts, cols)
    got = lax.all_to_all(term, ("q", "tp"), 0, 0, tiled=True)
    got = got.reshape(quads, parts, rows, group // parts, cols).astype(jnp.float32)
    total = jnp.sum(got, axis=1)
    total = total.transpose(1, 2, 0, 3).reshape(rows, (group // parts) * quads * cols)
    branch = total.astype(jnp.bfloat16).astype(jnp.float32)

    base = slot * tiles
    row_pos = jnp.concatenate(
        [base + jnp.arange(tiles, dtype=jnp.int32), jnp.stack([base - 1, base + tiles])]
    )
    row_valid = (row_pos >= 0) & (row_pos < my_len) & (row_pos < group * tiles)
    branch = jnp.where(row_valid[:, None], branch, 0.0)
    own = branch[:tiles]
    prev_rows = jnp.concatenate([branch[tiles : tiles + 1], own[:-1]], axis=0)
    next_rows = jnp.concatenate([own[1:], branch[tiles + 1 : tiles + 2]], axis=0)
    vel = own + mix_coef[None, :] * (prev_rows + next_rows - 2.0 * own)
    vel = jnp.where(row_valid[:tiles, None], vel, 0.0)
    frac = 1.0 - my_step.astype(jnp.float32) / STEPS
    sigma = 5.0 * frac / (1.0 + 4.0 * frac)
    updated = latent.astype(jnp.float32) + sigma * vel
    return (vel.astype(jnp.bfloat16), updated)


def solution(mesh):
    req = mesh.shape["req"]
    devices = mesh.devices.reshape(req // TENANTS, TENANTS, mesh.shape["tp"])
    split = Mesh(devices, ("z", "q", "tp"))
    rows = ("z", "q")
    placed = (
        P(rows, "tp"),
        P(rows, "tp"),
        P(rows, "tp"),
        P(rows, "tp"),
        P(rows, "tp"),
        P(rows, "tp"),
        P("tp", rows),
        P("tp", rows),
        P(),
        P("tp"),
        P(rows, "tp"),
        P(),
        P(),
        P(),
    )
    return jax.shard_map(
        shards,
        mesh=split,
        in_specs=placed,
        out_specs=(P(rows, "tp"), P(rows, "tp")),
        check_vma=False,
    )
```

```python
import jax
import jax.numpy as jnp
from jax import lax
from jax.experimental import pallas as pl
from jax.experimental.pallas import tpu as pltpu
from jax.sharding import Mesh, PartitionSpec as P

DH = 128
TENANTS = 4
STEPS = 50


def attend(q_rows, keys, values, valid):
    rows, feat = q_rows.shape
    heads = feat // DH
    q_heads = q_rows.reshape(rows, heads, DH)
    k_heads = keys.reshape(keys.shape[0], heads, DH)
    v_heads = values.reshape(values.shape[0], heads, DH)
    scores = jnp.einsum("qhd,khd->hqk", q_heads, k_heads, preferred_element_type=jnp.float32) * (
        1.0 / DH**0.5
    )
    scores = jnp.where(valid[None, None, :], scores, -1e30)
    top = jnp.max(scores, axis=-1, keepdims=True)
    weights = jnp.where(valid[None, None, :], jnp.exp(scores - top), 0.0)
    denom = jnp.sum(weights, axis=-1)
    mixed = jnp.einsum(
        "hqk,khd->hqd", weights.astype(jnp.bfloat16), v_heads, preferred_element_type=jnp.float32
    )
    out = mixed / denom[..., None]
    return out.transpose(1, 0, 2).reshape(rows, feat).astype(jnp.bfloat16)


def attention_pair(lens, q_rows, cq_rows, blocks, *, tiles, text_rows):
    group = len(blocks)
    rows, feat = q_rows.shape
    heads = feat // DH
    scale = 1.0 / DH**0.5
    t_at = 2 * tiles

    def one(q_ref, bufs, valid_of, k_off, v_off, width, o_ref, which):
        oks = [valid_of(j) for j in range(group)]
        for h in range(heads):
            lanes = pl.ds(h * DH, DH)
            q_h = q_ref[:, lanes]
            blocks = []
            for j in range(group):
                k_j = bufs[j][pl.ds(k_off, width), lanes]
                s = lax.dot_general(q_h, k_j, (((1,), (1,)), ((), ())), preferred_element_type=jnp.float32)
                blocks.append(jnp.where(oks[j], s * scale, -1e30))
            m = blocks[0].max(axis=-1, keepdims=True)
            for s in blocks[1:]:
                m = jnp.maximum(m, s.max(axis=-1, keepdims=True))
            den = jnp.zeros((rows, 1), jnp.float32)
            acc = jnp.zeros((rows, DH), jnp.float32)
            for j, s in enumerate(blocks):
                p = jnp.where(oks[j], jnp.exp(s - m), 0.0)
                v_j = bufs[j][pl.ds(v_off, width), lanes]
                den = den + jnp.sum(p, axis=-1, keepdims=True)
                acc = acc + jnp.dot(p.astype(jnp.bfloat16), v_j, preferred_element_type=jnp.float32)
            o_ref[which, :, lanes] = (acc / den).astype(o_ref.dtype)

    def kernel(lens_ref, q_ref, cq_ref, *refs):
        bufs, o_ref = refs[:-1], refs[-1]
        n_keys = lens_ref[0]
        n_text = lens_ref[1]
        here = lens_ref[2]

        def self_valid(j):
            pos = (here + j) % group * tiles + lax.broadcasted_iota(jnp.int32, (1, tiles), 1)
            return pos < n_keys

        def text_valid(j):
            pos = (here + j) % group * text_rows + lax.broadcasted_iota(jnp.int32, (1, text_rows), 1)
            return pos < n_text

        one(q_ref, bufs, self_valid, 0, tiles, tiles, o_ref, 0)
        one(cq_ref, bufs, text_valid, t_at, t_at + text_rows, text_rows, o_ref, 1)

    vmem = pltpu.MemorySpace.VMEM
    return pl.pallas_call(
        kernel,
        out_shape=jax.ShapeDtypeStruct((2, rows, feat), jnp.bfloat16),
        in_specs=[
            pl.BlockSpec(memory_space=pltpu.MemorySpace.SMEM),
            pl.BlockSpec(memory_space=vmem),
            pl.BlockSpec(memory_space=vmem),
        ]
        + [pl.BlockSpec(memory_space=vmem)] * group,
        out_specs=pl.BlockSpec(memory_space=vmem),
    )(lens, q_rows, cq_rows, *blocks)

def pack_block(key, value, text_key, text_value, w_self_t, w_cross_t, query, cross_query):
    pieces = (key, value, text_key, text_value, w_self_t, w_cross_t)
    starts = [0]
    for piece in pieces:
        starts.append(starts[-1] + piece.shape[0])
    edge_rows = 16
    feat = key.shape[1]
    last = query.shape[0] - 1

    def kernel(k_ref, v_ref, tk_ref, tv_ref, ws_ref, wc_ref, q_ref, cq_ref, o_ref):
        refs = (k_ref, v_ref, tk_ref, tv_ref, ws_ref, wc_ref)
        for ref, at in zip(refs, starts):
            o_ref[pl.ds(at, ref.shape[0]), :] = ref[...]
        q = q_ref[...].astype(jnp.float32)
        cq = cq_ref[...].astype(jnp.float32)
        row = lax.broadcasted_iota(jnp.int32, (edge_rows, feat), 0)
        edges = jnp.where(row == 0, q[0:1], 0.0)
        edges = jnp.where(row == 1, q[last : last + 1], edges)
        edges = jnp.where(row == 2, cq[0:1], edges)
        edges = jnp.where(row == 3, cq[last : last + 1], edges)
        o_ref[pl.ds(starts[-1], edge_rows), :] = edges.astype(o_ref.dtype)

    vmem = pltpu.MemorySpace.VMEM
    return pl.pallas_call(
        kernel,
        out_shape=jax.ShapeDtypeStruct((starts[-1] + edge_rows, feat), key.dtype),
        in_specs=[pl.BlockSpec(memory_space=vmem)] * 8,
        out_specs=pl.BlockSpec(memory_space=vmem),
    )(key, value, text_key, text_value, w_self_t, w_cross_t, query, cross_query)


def shards(
    query,
    key,
    value,
    cross_query,
    text_key,
    text_value,
    wo_self,
    wo_cross,
    attn_gate,
    mix_coef,
    latent,
    tenant_len,
    text_len,
    t_index,
):
    tiles, feat = query.shape
    text_rows = text_key.shape[0]
    cols = wo_self.shape[1]
    group = lax.axis_size("z")
    quads = lax.axis_size("q")
    parts = lax.axis_size("tp")
    slot = lax.axis_index("z")
    tenant = lax.axis_index("q")
    picker = jnp.arange(TENANTS) == tenant
    my_len = jnp.sum(jnp.where(picker, tenant_len, 0))
    my_text = jnp.sum(jnp.where(picker, text_len, 0))
    my_step = jnp.sum(jnp.where(picker, t_index, 0))

    packed = pack_block(key, value, text_key, text_value, wo_self.T, wo_cross.T, query, cross_query)
    ahead = [(i, (i + 1) % group) for i in range(group)]
    behind = [(i, (i - 1) % group) for i in range(group)]
    forward, backward = [packed], [packed]
    for t in range(1, group // 2 + 1):
        forward.append(lax.ppermute(forward[-1], "z", ahead))
        if t < group - group // 2:
            backward.append(lax.ppermute(backward[-1], "z", behind))
    blocks = backward + forward[len(forward) - 1 : 0 : -1]
    at = 2 * tiles + 2 * text_rows
    w_rot = jnp.stack([b[at : at + 2 * cols] for b in blocks])
    w_all = lax.dynamic_slice_in_dim(jnp.concatenate([w_rot, w_rot]), (group - slot) % group, group, 0)
    w_self_t = w_all[:, :cols]
    w_cross_t = w_all[:, cols:]
    at += 2 * cols
    prev_block, next_block = forward[1], backward[1]

    pad = (-(tiles + 2)) % 16
    q_rows = jnp.concatenate([query, prev_block[at + 1 : at + 2], next_block[at : at + 1]], axis=0)
    cq_rows = jnp.concatenate([cross_query, prev_block[at + 3 : at + 4], next_block[at + 2 : at + 3]], axis=0)
    q_rows = jnp.pad(q_rows, ((0, pad), (0, 0)))
    cq_rows = jnp.pad(cq_rows, ((0, pad), (0, 0)))
    lens = jnp.stack([my_len, my_text, slot]).astype(jnp.int32)
    a_pair = attention_pair(
        lens,
        q_rows,
        cq_rows,
        blocks,
        tiles=tiles,
        text_rows=text_rows,
    )

    a_all = lax.all_gather(a_pair, "q", axis=0, tiled=False)[:, :, : tiles + 2]
    rows = tiles + 2
    gate = attn_gate.reshape(TENANTS, group, quads, cols)
    gate = lax.dynamic_index_in_dim(gate, tenant, axis=2, keepdims=False).reshape(TENANTS, group * cols)
    s_term = jnp.einsum("qrd,kcd->qrkc", a_all[:, 0], w_self_t, preferred_element_type=jnp.float32)
    c_term = jnp.einsum("qrd,kcd->qrkc", a_all[:, 1], w_cross_t, preferred_element_type=jnp.float32)
    s_term = s_term.reshape(quads, rows, group * cols)
    c_term = c_term.reshape(quads, rows, group * cols)
    term = (gate[:, None, :] * s_term + c_term).astype(jnp.bfloat16)
    term = term.reshape(quads, rows, parts, group // parts, cols).transpose(0, 2, 1, 3, 4)
    term = term.reshape(quads * parts, rows, group // parts, cols)
    got = lax.all_to_all(term, ("q", "tp"), 0, 0, tiled=True)
    got = got.reshape(quads, parts, rows, group // parts, cols).astype(jnp.float32)
    total = jnp.sum(got, axis=1)
    total = total.transpose(1, 2, 0, 3).reshape(rows, (group // parts) * quads * cols)
    branch = total.astype(jnp.bfloat16).astype(jnp.float32)

    base = slot * tiles
    row_pos = jnp.concatenate(
        [base + jnp.arange(tiles, dtype=jnp.int32), jnp.stack([base - 1, base + tiles])]
    )
    row_valid = (row_pos >= 0) & (row_pos < my_len) & (row_pos < group * tiles)
    branch = jnp.where(row_valid[:, None], branch, 0.0)
    own = branch[:tiles]
    prev_rows = jnp.concatenate([branch[tiles : tiles + 1], own[:-1]], axis=0)
    next_rows = jnp.concatenate([own[1:], branch[tiles + 1 : tiles + 2]], axis=0)
    vel = own + mix_coef[None, :] * (prev_rows + next_rows - 2.0 * own)
    vel = jnp.where(row_valid[:tiles, None], vel, 0.0)
    frac = 1.0 - my_step.astype(jnp.float32) / STEPS
    sigma = 5.0 * frac / (1.0 + 4.0 * frac)
    updated = latent.astype(jnp.float32) + sigma * vel
    return (vel.astype(jnp.bfloat16), updated)


def solution(mesh):
    req = mesh.shape["req"]
    devices = mesh.devices.reshape(req // TENANTS, TENANTS, mesh.shape["tp"])
    split = Mesh(devices, ("z", "q", "tp"))
    rows = ("z", "q")
    placed = (
        P(rows, "tp"),
        P(rows, "tp"),
        P(rows, "tp"),
        P(rows, "tp"),
        P(rows, "tp"),
        P(rows, "tp"),
        P("tp", rows),
        P("tp", rows),
        P(),
        P("tp"),
        P(rows, "tp"),
        P(),
        P(),
        P(),
    )
    return jax.shard_map(
        shards,
        mesh=split,
        in_specs=placed,
        out_specs=(P(rows, "tp"), P(rows, "tp")),
        check_vma=False,
    )
```

```python
import jax
import jax.numpy as jnp
from jax import lax
from jax.experimental import pallas as pl
from jax.experimental.pallas import tpu as pltpu
from jax.sharding import Mesh, PartitionSpec as P

DH = 128
TENANTS = 4
STEPS = 50


def attention_pair(lens, q_rows, cq_rows, gathered, *, group, tiles, text_rows, stride):
    rows, feat = q_rows.shape
    heads = feat // DH
    scale = 1.0 / DH**0.5
    t_at = 2 * tiles

    def attend_all(q_ref, k_ref, v_ref, ok, o_ref, which):
        for h in range(heads):
            lanes = pl.ds(h * DH, DH)
            s = lax.dot_general(
                q_ref[:, lanes], k_ref[:, lanes], (((1,), (1,)), ((), ())), preferred_element_type=jnp.float32
            )
            s = jnp.where(ok, s * scale, -1e30)
            m = s.max(axis=-1, keepdims=True)
            p = jnp.where(ok, jnp.exp(s - m), 0.0)
            den = jnp.sum(p, axis=-1, keepdims=True)
            acc = jnp.dot(p.astype(jnp.bfloat16), v_ref[:, lanes], preferred_element_type=jnp.float32)
            o_ref[which, :, lanes] = (acc / den).astype(o_ref.dtype)

    def kernel(lens_ref, q_ref, cq_ref, buf, o_ref, tk_ref, tv_ref, k_ref, v_ref):
        n_keys = lens_ref[0]
        n_text = lens_ref[1]

        self_valid = lax.broadcasted_iota(jnp.int32, (1, group * tiles), 1) < n_keys
        text_valid = lax.broadcasted_iota(jnp.int32, (1, group * text_rows), 1) < n_text

        for j in range(group):
            tk_ref[pl.ds(j * text_rows, text_rows), :] = buf[pl.ds(j * stride + t_at, text_rows), :]
            tv_ref[pl.ds(j * text_rows, text_rows), :] = buf[pl.ds(j * stride + t_at + text_rows, text_rows), :]
        for j in range(group):
            k_ref[pl.ds(j * tiles, tiles), :] = buf[pl.ds(j * stride, tiles), :]
            v_ref[pl.ds(j * tiles, tiles), :] = buf[pl.ds(j * stride + tiles, tiles), :]
        attend_all(q_ref, k_ref, v_ref, self_valid, o_ref, 0)
        attend_all(cq_ref, tk_ref, tv_ref, text_valid, o_ref, 1)

    vmem = pltpu.MemorySpace.VMEM
    return pl.pallas_call(
        kernel,
        out_shape=jax.ShapeDtypeStruct((2, rows, feat), jnp.bfloat16),
        in_specs=[
            pl.BlockSpec(memory_space=pltpu.MemorySpace.SMEM),
            pl.BlockSpec(memory_space=vmem),
            pl.BlockSpec(memory_space=vmem),
            pl.BlockSpec(memory_space=vmem),
        ],
        out_specs=pl.BlockSpec(memory_space=vmem),
        scratch_shapes=[pltpu.VMEM((group * text_rows, feat), gathered.dtype)] * 2
        + [pltpu.VMEM((group * tiles, feat), gathered.dtype)] * 2,
    )(lens, q_rows, cq_rows, gathered)


def pack_block(key, value, text_key, text_value, w_self_t, w_cross_t, query, cross_query):
    pieces = (key, value, text_key, text_value, w_self_t, w_cross_t)
    starts = [0]
    for piece in pieces:
        starts.append(starts[-1] + piece.shape[0])
    edge_rows = 16
    feat = key.shape[1]
    last = query.shape[0] - 1

    def kernel(k_ref, v_ref, tk_ref, tv_ref, ws_ref, wc_ref, q_ref, cq_ref, o_ref):
        refs = (k_ref, v_ref, tk_ref, tv_ref, ws_ref, wc_ref)
        for ref, at in zip(refs, starts):
            o_ref[pl.ds(at, ref.shape[0]), :] = ref[...]
        q = q_ref[...].astype(jnp.float32)
        cq = cq_ref[...].astype(jnp.float32)
        row = lax.broadcasted_iota(jnp.int32, (edge_rows, feat), 0)
        edges = jnp.where(row == 0, q[0:1], 0.0)
        edges = jnp.where(row == 1, q[last : last + 1], edges)
        edges = jnp.where(row == 2, cq[0:1], edges)
        edges = jnp.where(row == 3, cq[last : last + 1], edges)
        o_ref[pl.ds(starts[-1], edge_rows), :] = edges.astype(o_ref.dtype)

    vmem = pltpu.MemorySpace.VMEM
    return pl.pallas_call(
        kernel,
        out_shape=jax.ShapeDtypeStruct((starts[-1] + edge_rows, feat), key.dtype),
        in_specs=[pl.BlockSpec(memory_space=vmem)] * 8,
        out_specs=pl.BlockSpec(memory_space=vmem),
    )(key, value, text_key, text_value, w_self_t, w_cross_t, query, cross_query)


def shards(
    query,
    key,
    value,
    cross_query,
    text_key,
    text_value,
    wo_self,
    wo_cross,
    attn_gate,
    mix_coef,
    latent,
    tenant_len,
    text_len,
    t_index,
):
    tiles, feat = query.shape
    text_rows = text_key.shape[0]
    cols = wo_self.shape[1]
    group = lax.axis_size("z")
    quads = lax.axis_size("q")
    parts = lax.axis_size("tp")
    slot = lax.axis_index("z")
    tenant = lax.axis_index("q")
    picker = jnp.arange(TENANTS) == tenant
    my_len = jnp.sum(jnp.where(picker, tenant_len, 0))
    my_text = jnp.sum(jnp.where(picker, text_len, 0))
    my_step = jnp.sum(jnp.where(picker, t_index, 0))

    packed = pack_block(key, value, text_key, text_value, wo_self.T, wo_cross.T, query, cross_query)
    gathered = lax.all_gather(packed, "z", axis=0, tiled=False)
    stride = gathered.shape[1]
    at = 2 * tiles + 2 * text_rows
    w_self_t = gathered[:, at : at + cols]
    at += cols
    w_cross_t = gathered[:, at : at + cols]
    at += cols
    e_g = gathered[:, at : at + 4]
    before = (slot + group - 1) % group
    after = (slot + 1) % group
    prev_edge = lax.dynamic_index_in_dim(e_g, before, axis=0, keepdims=False)
    next_edge = lax.dynamic_index_in_dim(e_g, after, axis=0, keepdims=False)
    pad = (-(tiles + 2)) % 16
    q_rows = jnp.concatenate([query, prev_edge[1:2], next_edge[0:1]], axis=0)
    cq_rows = jnp.concatenate([cross_query, prev_edge[3:4], next_edge[2:3]], axis=0)
    q_rows = jnp.pad(q_rows, ((0, pad), (0, 0)))
    cq_rows = jnp.pad(cq_rows, ((0, pad), (0, 0)))
    lens = jnp.stack([my_len, my_text]).astype(jnp.int32)
    a_pair = attention_pair(
        lens,
        q_rows,
        cq_rows,
        gathered.reshape(group * stride, feat),
        group=group,
        tiles=tiles,
        text_rows=text_rows,
        stride=stride,
    )

    w_self = w_self_t.transpose(2, 0, 1).reshape(feat, group * cols)
    w_cross = w_cross_t.transpose(2, 0, 1).reshape(feat, group * cols)

    a_all = lax.all_gather(a_pair, "q", axis=0, tiled=False)[:, :, : tiles + 2]
    rows = tiles + 2
    gate = attn_gate.reshape(TENANTS, group, quads, cols)
    gate = lax.dynamic_index_in_dim(gate, tenant, axis=2, keepdims=False).reshape(TENANTS, group * cols)
    s_term = jnp.einsum("qrd,dc->qrc", a_all[:, 0], w_self, preferred_element_type=jnp.float32)
    c_term = jnp.einsum("qrd,dc->qrc", a_all[:, 1], w_cross, preferred_element_type=jnp.float32)
    term = (gate[:, None, :] * s_term + c_term).astype(jnp.bfloat16)
    term = term.reshape(quads, rows, parts, group // parts, cols).transpose(0, 2, 1, 3, 4)
    term = term.reshape(quads * parts, rows, group // parts, cols)
    got = lax.all_to_all(term, ("q", "tp"), 0, 0, tiled=True)
    got = got.reshape(quads, parts, rows, group // parts, cols).astype(jnp.float32)
    total = jnp.sum(got, axis=1)
    total = total.transpose(1, 2, 0, 3).reshape(rows, (group // parts) * quads * cols)
    branch = total.astype(jnp.bfloat16).astype(jnp.float32)

    base = slot * tiles
    row_pos = jnp.concatenate(
        [base + jnp.arange(tiles, dtype=jnp.int32), jnp.stack([base - 1, base + tiles])]
    )
    row_valid = (row_pos >= 0) & (row_pos < my_len) & (row_pos < group * tiles)
    branch = jnp.where(row_valid[:, None], branch, 0.0)
    own = branch[:tiles]
    prev_rows = jnp.concatenate([branch[tiles : tiles + 1], own[:-1]], axis=0)
    next_rows = jnp.concatenate([own[1:], branch[tiles + 1 : tiles + 2]], axis=0)
    vel = own + mix_coef[None, :] * (prev_rows + next_rows - 2.0 * own)
    vel = jnp.where(row_valid[:tiles, None], vel, 0.0)
    frac = 1.0 - my_step.astype(jnp.float32) / STEPS
    sigma = 5.0 * frac / (1.0 + 4.0 * frac)
    updated = latent.astype(jnp.float32) + sigma * vel
    return (vel.astype(jnp.bfloat16), updated)


def solution(mesh):
    req = mesh.shape["req"]
    devices = mesh.devices.reshape(req // TENANTS, TENANTS, mesh.shape["tp"])
    split = Mesh(devices, ("z", "q", "tp"))
    rows = ("z", "q")
    placed = (
        P(rows, "tp"),
        P(rows, "tp"),
        P(rows, "tp"),
        P(rows, "tp"),
        P(rows, "tp"),
        P(rows, "tp"),
        P("tp", rows),
        P("tp", rows),
        P(),
        P("tp"),
        P(rows, "tp"),
        P(),
        P(),
        P(),
    )
    return jax.shard_map(
        shards,
        mesh=split,
        in_specs=placed,
        out_specs=(P(rows, "tp"), P(rows, "tp")),
        check_vma=False,
    )
```

```python
import jax
import jax.numpy as jnp
from jax import lax
from jax.experimental import pallas as pl
from jax.experimental.pallas import tpu as pltpu
from jax.sharding import Mesh, PartitionSpec as P

DH = 128
TENANTS = 4
STEPS = 50


def attention_pair(lens, query, cross_query, gathered, *, group, tiles, text_rows, stride, edge_at):
    feat = query.shape[1]
    rows = tiles + 16
    heads = feat // DH
    scale = 1.0 / DH**0.5
    t_at = 2 * tiles

    def attend_all(q_ref, k_ref, v_ref, ok, o_ref, which):
        for h in range(heads):
            lanes = pl.ds(h * DH, DH)
            s = lax.dot_general(
                q_ref[:, lanes], k_ref[:, lanes], (((1,), (1,)), ((), ())), preferred_element_type=jnp.float32
            )
            s = jnp.where(ok, s * scale, -1e30)
            m = s.max(axis=-1, keepdims=True)
            p = jnp.where(ok, jnp.exp(s - m), 0.0)
            den = jnp.sum(p, axis=-1, keepdims=True)
            acc = jnp.dot(p.astype(jnp.bfloat16), v_ref[:, lanes], preferred_element_type=jnp.float32)
            o_ref[which, :, lanes] = (acc / den).astype(o_ref.dtype)

    def kernel(lens_ref, query_ref, cquery_ref, buf, o_ref, tk_ref, tv_ref, k_ref, v_ref, q_ref, cq_ref):
        n_keys = lens_ref[0]
        n_text = lens_ref[1]
        before = buf[pl.ds(pl.multiple_of(lens_ref[2] * stride + edge_at, 16), 16), :].astype(jnp.float32)
        after = buf[pl.ds(pl.multiple_of(lens_ref[3] * stride + edge_at, 16), 16), :].astype(jnp.float32)
        row = lax.broadcasted_iota(jnp.int32, (16, feat), 0)
        q_ref[pl.ds(0, tiles), :] = query_ref[...]
        cq_ref[pl.ds(0, tiles), :] = cquery_ref[...]
        q_tail = jnp.where(row == 0, before[1:2], jnp.where(row == 1, after[0:1], 0.0))
        cq_tail = jnp.where(row == 0, before[3:4], jnp.where(row == 1, after[2:3], 0.0))
        q_ref[pl.ds(tiles, 16), :] = q_tail.astype(q_ref.dtype)
        cq_ref[pl.ds(tiles, 16), :] = cq_tail.astype(cq_ref.dtype)

        self_valid = lax.broadcasted_iota(jnp.int32, (1, group * tiles), 1) < n_keys
        text_valid = lax.broadcasted_iota(jnp.int32, (1, group * text_rows), 1) < n_text

        for j in range(group):
            tk_ref[pl.ds(j * text_rows, text_rows), :] = buf[pl.ds(j * stride + t_at, text_rows), :]
            tv_ref[pl.ds(j * text_rows, text_rows), :] = buf[pl.ds(j * stride + t_at + text_rows, text_rows), :]
        for j in range(group):
            k_ref[pl.ds(j * tiles, tiles), :] = buf[pl.ds(j * stride, tiles), :]
            v_ref[pl.ds(j * tiles, tiles), :] = buf[pl.ds(j * stride + tiles, tiles), :]
        attend_all(q_ref, k_ref, v_ref, self_valid, o_ref, 0)
        attend_all(cq_ref, tk_ref, tv_ref, text_valid, o_ref, 1)

    vmem = pltpu.MemorySpace.VMEM
    return pl.pallas_call(
        kernel,
        out_shape=jax.ShapeDtypeStruct((2, rows, feat), jnp.bfloat16),
        in_specs=[
            pl.BlockSpec(memory_space=pltpu.MemorySpace.SMEM),
            pl.BlockSpec(memory_space=vmem),
            pl.BlockSpec(memory_space=vmem),
            pl.BlockSpec(memory_space=vmem),
        ],
        out_specs=pl.BlockSpec(memory_space=vmem),
        scratch_shapes=[pltpu.VMEM((group * text_rows, feat), gathered.dtype)] * 2
        + [pltpu.VMEM((group * tiles, feat), gathered.dtype)] * 2
        + [pltpu.VMEM((rows, feat), query.dtype)] * 2,
    )(lens, query, cross_query, gathered)


def pack_block(key, value, text_key, text_value, w_self_t, w_cross_t, query, cross_query):
    pieces = (key, value, text_key, text_value, w_self_t, w_cross_t)
    starts = [0]
    for piece in pieces:
        starts.append(starts[-1] + piece.shape[0])
    edge_rows = 16
    feat = key.shape[1]
    last = query.shape[0] - 1

    def kernel(k_ref, v_ref, tk_ref, tv_ref, ws_ref, wc_ref, q_ref, cq_ref, o_ref):
        refs = (k_ref, v_ref, tk_ref, tv_ref, ws_ref, wc_ref)
        for ref, at in zip(refs, starts):
            o_ref[pl.ds(at, ref.shape[0]), :] = ref[...]
        q = q_ref[...].astype(jnp.float32)
        cq = cq_ref[...].astype(jnp.float32)
        row = lax.broadcasted_iota(jnp.int32, (edge_rows, feat), 0)
        edges = jnp.where(row == 0, q[0:1], 0.0)
        edges = jnp.where(row == 1, q[last : last + 1], edges)
        edges = jnp.where(row == 2, cq[0:1], edges)
        edges = jnp.where(row == 3, cq[last : last + 1], edges)
        o_ref[pl.ds(starts[-1], edge_rows), :] = edges.astype(o_ref.dtype)

    vmem = pltpu.MemorySpace.VMEM
    return pl.pallas_call(
        kernel,
        out_shape=jax.ShapeDtypeStruct((starts[-1] + edge_rows, feat), key.dtype),
        in_specs=[pl.BlockSpec(memory_space=vmem)] * 8,
        out_specs=pl.BlockSpec(memory_space=vmem),
    )(key, value, text_key, text_value, w_self_t, w_cross_t, query, cross_query)


def shards(
    query,
    key,
    value,
    cross_query,
    text_key,
    text_value,
    wo_self,
    wo_cross,
    attn_gate,
    mix_coef,
    latent,
    tenant_len,
    text_len,
    t_index,
):
    tiles, feat = query.shape
    text_rows = text_key.shape[0]
    cols = wo_self.shape[1]
    group = lax.axis_size("z")
    quads = lax.axis_size("q")
    parts = lax.axis_size("tp")
    slot = lax.axis_index("z")
    tenant = lax.axis_index("q")
    picker = jnp.arange(TENANTS) == tenant
    my_len = jnp.sum(jnp.where(picker, tenant_len, 0))
    my_text = jnp.sum(jnp.where(picker, text_len, 0))
    my_step = jnp.sum(jnp.where(picker, t_index, 0))

    packed = pack_block(key, value, text_key, text_value, wo_self.T, wo_cross.T, query, cross_query)
    gathered = lax.all_gather(packed, "z", axis=0, tiled=False)
    stride = gathered.shape[1]
    at = 2 * tiles + 2 * text_rows
    w_self_t = gathered[:, at : at + cols]
    at += cols
    w_cross_t = gathered[:, at : at + cols]
    at += cols
    before = (slot + group - 1) % group
    after = (slot + 1) % group
    lens = jnp.stack([my_len, my_text, before, after]).astype(jnp.int32)
    a_pair = attention_pair(
        lens,
        query,
        cross_query,
        gathered.reshape(group * stride, feat),
        group=group,
        tiles=tiles,
        text_rows=text_rows,
        stride=stride,
        edge_at=at,
    )

    w_self = w_self_t.transpose(2, 0, 1).reshape(feat, group * cols)
    w_cross = w_cross_t.transpose(2, 0, 1).reshape(feat, group * cols)

    a_all = lax.all_gather(a_pair, "q", axis=0, tiled=False)[:, :, : tiles + 2]
    rows = tiles + 2
    gate = attn_gate.reshape(TENANTS, group, quads, cols)
    gate = lax.dynamic_index_in_dim(gate, tenant, axis=2, keepdims=False).reshape(TENANTS, group * cols)
    s_term = jnp.einsum("qrd,dc->qrc", a_all[:, 0], w_self, preferred_element_type=jnp.float32)
    c_term = jnp.einsum("qrd,dc->qrc", a_all[:, 1], w_cross, preferred_element_type=jnp.float32)
    term = (gate[:, None, :] * s_term + c_term).astype(jnp.bfloat16)
    term = term.reshape(quads, rows, parts, group // parts, cols).transpose(0, 2, 1, 3, 4)
    term = term.reshape(quads * parts, rows, group // parts, cols)
    got = lax.all_to_all(term, ("q", "tp"), 0, 0, tiled=True)
    got = got.reshape(quads, parts, rows, group // parts, cols).astype(jnp.float32)
    total = jnp.sum(got, axis=1)
    total = total.transpose(1, 2, 0, 3).reshape(rows, (group // parts) * quads * cols)
    branch = total.astype(jnp.bfloat16).astype(jnp.float32)

    base = slot * tiles
    row_pos = jnp.concatenate(
        [base + jnp.arange(tiles, dtype=jnp.int32), jnp.stack([base - 1, base + tiles])]
    )
    row_valid = (row_pos >= 0) & (row_pos < my_len) & (row_pos < group * tiles)
    branch = jnp.where(row_valid[:, None], branch, 0.0)
    own = branch[:tiles]
    prev_rows = jnp.concatenate([branch[tiles : tiles + 1], own[:-1]], axis=0)
    next_rows = jnp.concatenate([own[1:], branch[tiles + 1 : tiles + 2]], axis=0)
    vel = own + mix_coef[None, :] * (prev_rows + next_rows - 2.0 * own)
    vel = jnp.where(row_valid[:tiles, None], vel, 0.0)
    frac = 1.0 - my_step.astype(jnp.float32) / STEPS
    sigma = 5.0 * frac / (1.0 + 4.0 * frac)
    updated = latent.astype(jnp.float32) + sigma * vel
    return (vel.astype(jnp.bfloat16), updated)


def solution(mesh):
    req = mesh.shape["req"]
    devices = mesh.devices.reshape(req // TENANTS, TENANTS, mesh.shape["tp"])
    split = Mesh(devices, ("z", "q", "tp"))
    rows = ("z", "q")
    placed = (
        P(rows, "tp"),
        P(rows, "tp"),
        P(rows, "tp"),
        P(rows, "tp"),
        P(rows, "tp"),
        P(rows, "tp"),
        P("tp", rows),
        P("tp", rows),
        P(),
        P("tp"),
        P(rows, "tp"),
        P(),
        P(),
        P(),
    )
    return jax.shard_map(
        shards,
        mesh=split,
        in_specs=placed,
        out_specs=(P(rows, "tp"), P(rows, "tp")),
        check_vma=False,
    )
```

```python
import jax
import jax.numpy as jnp
from jax import lax
from jax.experimental import pallas as pl
from jax.experimental.pallas import tpu as pltpu
from jax.sharding import Mesh, PartitionSpec as P

DH = 128
TENANTS = 4
STEPS = 50


def attention_pair(lens, query, cross_query, blocks, *, tiles, text_rows, cols):
    group = len(blocks)
    feat = query.shape[1]
    rows = tiles + 16
    heads = feat // DH
    scale = 1.0 / DH**0.5
    t_at = 2 * tiles
    w_at = t_at + 2 * text_rows
    edge_at = w_at + 2 * cols

    def attend_all(q_ref, k_ref, v_ref, ok, o_ref, which):
        for h in range(heads):
            lanes = pl.ds(h * DH, DH)
            s = lax.dot_general(
                q_ref[:, lanes], k_ref[:, lanes], (((1,), (1,)), ((), ())), preferred_element_type=jnp.float32
            )
            s = jnp.where(ok, s * scale, -1e30)
            m = s.max(axis=-1, keepdims=True)
            p = jnp.where(ok, jnp.exp(s - m), 0.0)
            den = jnp.sum(p, axis=-1, keepdims=True)
            acc = jnp.dot(p.astype(jnp.bfloat16), v_ref[:, lanes], preferred_element_type=jnp.float32)
            o_ref[which, :, lanes] = (acc / den).astype(o_ref.dtype)

    def kernel(lens_ref, query_ref, cquery_ref, *refs):
        bufs = refs[:group]
        o_ref, w_ref, tk_ref, tv_ref, k_ref, v_ref, q_ref, cq_ref = refs[group:]
        n_keys = lens_ref[0]
        n_text = lens_ref[1]
        here = lens_ref[2]
        before = bufs[group - 1][pl.ds(edge_at, 16), :].astype(jnp.float32)
        after = bufs[1][pl.ds(edge_at, 16), :].astype(jnp.float32)
        row = lax.broadcasted_iota(jnp.int32, (16, feat), 0)
        q_ref[pl.ds(0, tiles), :] = query_ref[...]
        cq_ref[pl.ds(0, tiles), :] = cquery_ref[...]
        q_tail = jnp.where(row == 0, before[1:2], jnp.where(row == 1, after[0:1], 0.0))
        cq_tail = jnp.where(row == 0, before[3:4], jnp.where(row == 1, after[2:3], 0.0))
        q_ref[pl.ds(tiles, 16), :] = q_tail.astype(q_ref.dtype)
        cq_ref[pl.ds(tiles, 16), :] = cq_tail.astype(cq_ref.dtype)

        self_valid = lax.broadcasted_iota(jnp.int32, (1, group * tiles), 1) < n_keys
        text_valid = lax.broadcasted_iota(jnp.int32, (1, group * text_rows), 1) < n_text

        for j in range(group):
            at = (here + j) % group
            buf = bufs[j]
            tk_ref[pl.ds(pl.multiple_of(at * text_rows, 16), text_rows), :] = buf[pl.ds(t_at, text_rows), :]
            tv_ref[pl.ds(pl.multiple_of(at * text_rows, 16), text_rows), :] = buf[
                pl.ds(t_at + text_rows, text_rows), :
            ]
            k_ref[pl.ds(pl.multiple_of(at * tiles, 16), tiles), :] = buf[pl.ds(0, tiles), :]
            v_ref[pl.ds(pl.multiple_of(at * tiles, 16), tiles), :] = buf[pl.ds(tiles, tiles), :]
            w_ref[0, pl.ds(pl.multiple_of(at * cols, 16), cols), :] = buf[pl.ds(w_at, cols), :]
            w_ref[1, pl.ds(pl.multiple_of(at * cols, 16), cols), :] = buf[pl.ds(w_at + cols, cols), :]
        attend_all(q_ref, k_ref, v_ref, self_valid, o_ref, 0)
        attend_all(cq_ref, tk_ref, tv_ref, text_valid, o_ref, 1)

    vmem = pltpu.MemorySpace.VMEM
    dtype = query.dtype
    return pl.pallas_call(
        kernel,
        out_shape=(
            jax.ShapeDtypeStruct((2, rows, feat), dtype),
            jax.ShapeDtypeStruct((2, group * cols, feat), dtype),
        ),
        in_specs=[pl.BlockSpec(memory_space=pltpu.MemorySpace.SMEM)]
        + [pl.BlockSpec(memory_space=vmem)] * (2 + group),
        out_specs=(pl.BlockSpec(memory_space=vmem), pl.BlockSpec(memory_space=vmem)),
        scratch_shapes=[pltpu.VMEM((group * text_rows, feat), dtype)] * 2
        + [pltpu.VMEM((group * tiles, feat), dtype)] * 2
        + [pltpu.VMEM((rows, feat), dtype)] * 2,
    )(lens, query, cross_query, *blocks)


def pack_block(key, value, text_key, text_value, w_self_t, w_cross_t, query, cross_query):
    pieces = (key, value, text_key, text_value, w_self_t, w_cross_t)
    starts = [0]
    for piece in pieces:
        starts.append(starts[-1] + piece.shape[0])
    edge_rows = 16
    feat = key.shape[1]
    last = query.shape[0] - 1

    def kernel(k_ref, v_ref, tk_ref, tv_ref, ws_ref, wc_ref, q_ref, cq_ref, o_ref):
        refs = (k_ref, v_ref, tk_ref, tv_ref, ws_ref, wc_ref)
        for ref, at in zip(refs, starts):
            o_ref[pl.ds(at, ref.shape[0]), :] = ref[...]
        q = q_ref[...].astype(jnp.float32)
        cq = cq_ref[...].astype(jnp.float32)
        row = lax.broadcasted_iota(jnp.int32, (edge_rows, feat), 0)
        edges = jnp.where(row == 0, q[0:1], 0.0)
        edges = jnp.where(row == 1, q[last : last + 1], edges)
        edges = jnp.where(row == 2, cq[0:1], edges)
        edges = jnp.where(row == 3, cq[last : last + 1], edges)
        o_ref[pl.ds(starts[-1], edge_rows), :] = edges.astype(o_ref.dtype)

    vmem = pltpu.MemorySpace.VMEM
    return pl.pallas_call(
        kernel,
        out_shape=jax.ShapeDtypeStruct((starts[-1] + edge_rows, feat), key.dtype),
        in_specs=[pl.BlockSpec(memory_space=vmem)] * 8,
        out_specs=pl.BlockSpec(memory_space=vmem),
    )(key, value, text_key, text_value, w_self_t, w_cross_t, query, cross_query)


def shards(
    query,
    key,
    value,
    cross_query,
    text_key,
    text_value,
    wo_self,
    wo_cross,
    attn_gate,
    mix_coef,
    latent,
    tenant_len,
    text_len,
    t_index,
):
    tiles, feat = query.shape
    text_rows = text_key.shape[0]
    cols = wo_self.shape[1]
    group = lax.axis_size("z")
    quads = lax.axis_size("q")
    parts = lax.axis_size("tp")
    slot = lax.axis_index("z")
    tenant = lax.axis_index("q")
    picker = jnp.arange(TENANTS) == tenant
    my_len = jnp.sum(jnp.where(picker, tenant_len, 0))
    my_text = jnp.sum(jnp.where(picker, text_len, 0))
    my_step = jnp.sum(jnp.where(picker, t_index, 0))

    packed = pack_block(key, value, text_key, text_value, wo_self.T, wo_cross.T, query, cross_query)
    ahead = [(i, (i + 1) % group) for i in range(group)]
    behind = [(i, (i - 1) % group) for i in range(group)]
    forward, backward = [packed], [packed]
    for t in range(1, group // 2 + 1):
        forward.append(lax.ppermute(forward[-1], "z", ahead))
        if t < group - group // 2:
            backward.append(lax.ppermute(backward[-1], "z", behind))
    blocks = backward + forward[len(forward) - 1 : 0 : -1]
    lens = jnp.stack([my_len, my_text, slot]).astype(jnp.int32)
    a_pair, w_all = attention_pair(lens, query, cross_query, blocks, tiles=tiles, text_rows=text_rows, cols=cols)

    a_all = lax.all_gather(a_pair, "q", axis=0, tiled=False)[:, :, : tiles + 2]
    rows = tiles + 2
    gate = attn_gate.reshape(TENANTS, group, quads, cols)
    gate = lax.dynamic_index_in_dim(gate, tenant, axis=2, keepdims=False).reshape(TENANTS, group * cols)
    s_term = jnp.einsum("qrd,cd->qrc", a_all[:, 0], w_all[0], preferred_element_type=jnp.float32)
    c_term = jnp.einsum("qrd,cd->qrc", a_all[:, 1], w_all[1], preferred_element_type=jnp.float32)
    term = (gate[:, None, :] * s_term + c_term).astype(jnp.bfloat16)
    term = term.reshape(quads, rows, parts, group // parts, cols).transpose(0, 2, 1, 3, 4)
    term = term.reshape(quads * parts, rows, group // parts, cols)
    got = lax.all_to_all(term, ("q", "tp"), 0, 0, tiled=True)
    got = got.reshape(quads, parts, rows, group // parts, cols).astype(jnp.float32)
    total = jnp.sum(got, axis=1)
    total = total.transpose(1, 2, 0, 3).reshape(rows, (group // parts) * quads * cols)
    branch = total.astype(jnp.bfloat16).astype(jnp.float32)

    base = slot * tiles
    row_pos = jnp.concatenate(
        [base + jnp.arange(tiles, dtype=jnp.int32), jnp.stack([base - 1, base + tiles])]
    )
    row_valid = (row_pos >= 0) & (row_pos < my_len) & (row_pos < group * tiles)
    branch = jnp.where(row_valid[:, None], branch, 0.0)
    own = branch[:tiles]
    prev_rows = jnp.concatenate([branch[tiles : tiles + 1], own[:-1]], axis=0)
    next_rows = jnp.concatenate([own[1:], branch[tiles + 1 : tiles + 2]], axis=0)
    vel = own + mix_coef[None, :] * (prev_rows + next_rows - 2.0 * own)
    vel = jnp.where(row_valid[:tiles, None], vel, 0.0)
    frac = 1.0 - my_step.astype(jnp.float32) / STEPS
    sigma = 5.0 * frac / (1.0 + 4.0 * frac)
    updated = latent.astype(jnp.float32) + sigma * vel
    return (vel.astype(jnp.bfloat16), updated)


def solution(mesh):
    req = mesh.shape["req"]
    devices = mesh.devices.reshape(req // TENANTS, TENANTS, mesh.shape["tp"])
    split = Mesh(devices, ("z", "q", "tp"))
    rows = ("z", "q")
    placed = (
        P(rows, "tp"),
        P(rows, "tp"),
        P(rows, "tp"),
        P(rows, "tp"),
        P(rows, "tp"),
        P(rows, "tp"),
        P("tp", rows),
        P("tp", rows),
        P(),
        P("tp"),
        P(rows, "tp"),
        P(),
        P(),
        P(),
    )
    return jax.shard_map(
        shards,
        mesh=split,
        in_specs=placed,
        out_specs=(P(rows, "tp"), P(rows, "tp")),
        check_vma=False,
    )
```

```python
import jax
import jax.numpy as jnp
from jax import lax
from jax.experimental import pallas as pl
from jax.experimental.pallas import tpu as pltpu
from jax.sharding import Mesh, PartitionSpec as P

DH = 128
TENANTS = 4
STEPS = 50


def attention_pair(lens, query, cross_query, blocks, *, tiles, text_rows, cols):
    group = len(blocks)
    feat = query.shape[1]
    rows = tiles + 16
    heads = feat // DH
    scale = 1.0 / DH**0.5
    t_at = 2 * tiles
    w_at = t_at + 2 * text_rows
    edge_at = w_at + 2 * cols

    def attend_all(q_ref, k_ref, v_ref, ok, o_ref, which):
        for h in range(heads):
            lanes = pl.ds(h * DH, DH)
            s = lax.dot_general(
                q_ref[:, lanes], k_ref[:, lanes], (((1,), (1,)), ((), ())), preferred_element_type=jnp.float32
            )
            s = jnp.where(ok, s * scale, -1e30)
            m = s.max(axis=-1, keepdims=True)
            p = jnp.where(ok, jnp.exp(s - m), 0.0)
            den = jnp.sum(p, axis=-1, keepdims=True)
            acc = jnp.dot(p.astype(jnp.bfloat16), v_ref[:, lanes], preferred_element_type=jnp.float32)
            o_ref[which, :, lanes] = (acc / den).astype(o_ref.dtype)

    flat = []
    for b in blocks:
        flat.extend(b if isinstance(b, tuple) else (b,))
    split = 2 * tiles

    def kernel(lens_ref, query_ref, cquery_ref, *refs):
        bufs, at_ref = [], 0
        for b in blocks:
            n = len(b) if isinstance(b, tuple) else 1
            bufs.append(refs[at_ref] if n == 1 else refs[at_ref : at_ref + n])
            at_ref += n
        o_ref, w_ref, tk_ref, tv_ref, k_ref, v_ref, q_ref, cq_ref = refs[at_ref:]

        def read(buf, start, size):
            if isinstance(buf, tuple):
                return buf[0][pl.ds(start, size), :] if start < split else buf[1][pl.ds(start - split, size), :]
            return buf[pl.ds(start, size), :]

        n_keys = lens_ref[0]
        n_text = lens_ref[1]
        here = lens_ref[2]
        before = read(bufs[group - 1], edge_at, 16).astype(jnp.float32)
        after = read(bufs[1], edge_at, 16).astype(jnp.float32)
        row = lax.broadcasted_iota(jnp.int32, (16, feat), 0)
        q_ref[pl.ds(0, tiles), :] = query_ref[...]
        cq_ref[pl.ds(0, tiles), :] = cquery_ref[...]
        q_tail = jnp.where(row == 0, before[1:2], jnp.where(row == 1, after[0:1], 0.0))
        cq_tail = jnp.where(row == 0, before[3:4], jnp.where(row == 1, after[2:3], 0.0))
        q_ref[pl.ds(tiles, 16), :] = q_tail.astype(q_ref.dtype)
        cq_ref[pl.ds(tiles, 16), :] = cq_tail.astype(cq_ref.dtype)

        self_valid = lax.broadcasted_iota(jnp.int32, (1, group * tiles), 1) < n_keys
        text_valid = lax.broadcasted_iota(jnp.int32, (1, group * text_rows), 1) < n_text

        for j in range(group):
            at = (here + j) % group
            buf = bufs[j]
            tk_ref[pl.ds(pl.multiple_of(at * text_rows, 16), text_rows), :] = read(buf, t_at, text_rows)
            tv_ref[pl.ds(pl.multiple_of(at * text_rows, 16), text_rows), :] = read(buf, t_at + text_rows, text_rows)
            k_ref[pl.ds(pl.multiple_of(at * tiles, 16), tiles), :] = read(buf, 0, tiles)
            v_ref[pl.ds(pl.multiple_of(at * tiles, 16), tiles), :] = read(buf, tiles, tiles)
            w_ref[0, pl.ds(pl.multiple_of(at * cols, 16), cols), :] = read(buf, w_at, cols)
            w_ref[1, pl.ds(pl.multiple_of(at * cols, 16), cols), :] = read(buf, w_at + cols, cols)
        attend_all(q_ref, k_ref, v_ref, self_valid, o_ref, 0)
        attend_all(cq_ref, tk_ref, tv_ref, text_valid, o_ref, 1)

    vmem = pltpu.MemorySpace.VMEM
    dtype = query.dtype
    return pl.pallas_call(
        kernel,
        out_shape=(
            jax.ShapeDtypeStruct((2, rows, feat), dtype),
            jax.ShapeDtypeStruct((2, group * cols, feat), dtype),
        ),
        in_specs=[pl.BlockSpec(memory_space=pltpu.MemorySpace.SMEM)]
        + [pl.BlockSpec(memory_space=vmem)] * (2 + len(flat)),
        out_specs=(pl.BlockSpec(memory_space=vmem), pl.BlockSpec(memory_space=vmem)),
        scratch_shapes=[pltpu.VMEM((group * text_rows, feat), dtype)] * 2
        + [pltpu.VMEM((group * tiles, feat), dtype)] * 2
        + [pltpu.VMEM((rows, feat), dtype)] * 2,
    )(lens, query, cross_query, *flat)


def pack_block(key, value, text_key, text_value, w_self_t, w_cross_t, query, cross_query):
    pieces = (key, value, text_key, text_value, w_self_t, w_cross_t)
    starts = [0]
    for piece in pieces:
        starts.append(starts[-1] + piece.shape[0])
    edge_rows = 16
    feat = key.shape[1]
    last = query.shape[0] - 1

    def kernel(k_ref, v_ref, tk_ref, tv_ref, ws_ref, wc_ref, q_ref, cq_ref, o_ref):
        refs = (k_ref, v_ref, tk_ref, tv_ref, ws_ref, wc_ref)
        for ref, at in zip(refs, starts):
            o_ref[pl.ds(at, ref.shape[0]), :] = ref[...]
        q = q_ref[...].astype(jnp.float32)
        cq = cq_ref[...].astype(jnp.float32)
        row = lax.broadcasted_iota(jnp.int32, (edge_rows, feat), 0)
        edges = jnp.where(row == 0, q[0:1], 0.0)
        edges = jnp.where(row == 1, q[last : last + 1], edges)
        edges = jnp.where(row == 2, cq[0:1], edges)
        edges = jnp.where(row == 3, cq[last : last + 1], edges)
        o_ref[pl.ds(starts[-1], edge_rows), :] = edges.astype(o_ref.dtype)

    vmem = pltpu.MemorySpace.VMEM
    return pl.pallas_call(
        kernel,
        out_shape=jax.ShapeDtypeStruct((starts[-1] + edge_rows, feat), key.dtype),
        in_specs=[pl.BlockSpec(memory_space=vmem)] * 8,
        out_specs=pl.BlockSpec(memory_space=vmem),
    )(key, value, text_key, text_value, w_self_t, w_cross_t, query, cross_query)


def shards(
    query,
    key,
    value,
    cross_query,
    text_key,
    text_value,
    wo_self,
    wo_cross,
    attn_gate,
    mix_coef,
    latent,
    tenant_len,
    text_len,
    t_index,
):
    tiles, feat = query.shape
    text_rows = text_key.shape[0]
    cols = wo_self.shape[1]
    group = lax.axis_size("z")
    quads = lax.axis_size("q")
    parts = lax.axis_size("tp")
    slot = lax.axis_index("z")
    tenant = lax.axis_index("q")
    picker = jnp.arange(TENANTS) == tenant
    my_len = jnp.sum(jnp.where(picker, tenant_len, 0))
    my_text = jnp.sum(jnp.where(picker, text_len, 0))
    my_step = jnp.sum(jnp.where(picker, t_index, 0))

    packed = pack_block(key, value, text_key, text_value, wo_self.T, wo_cross.T, query, cross_query)
    ahead = [(i, (i + 1) % group) for i in range(group)]
    behind = [(i, (i - 1) % group) for i in range(group)]
    forward, backward = [packed], [packed]
    split = 2 * tiles
    for t in range(1, group // 2 + 1):
        if 2 * t == group:
            forward.append(lax.ppermute(forward[-1][:split], "z", ahead))
            backward.append(lax.ppermute(backward[-1][split:], "z", behind))
            continue
        forward.append(lax.ppermute(forward[-1], "z", ahead))
        if t < group - group // 2:
            backward.append(lax.ppermute(backward[-1], "z", behind))
    if group % 2 == 0:
        middle = [(forward[group // 2], backward[group // 2])]
        blocks = backward[: group // 2] + middle + forward[group // 2 - 1 : 0 : -1]
    else:
        blocks = backward + forward[len(forward) - 1 : 0 : -1]
    lens = jnp.stack([my_len, my_text, slot]).astype(jnp.int32)
    a_pair, w_all = attention_pair(lens, query, cross_query, blocks, tiles=tiles, text_rows=text_rows, cols=cols)

    a_all = lax.all_gather(a_pair, "q", axis=0, tiled=False)[:, :, : tiles + 2]
    rows = tiles + 2
    gate = attn_gate.reshape(TENANTS, group, quads, cols)
    gate = lax.dynamic_index_in_dim(gate, tenant, axis=2, keepdims=False).reshape(TENANTS, group * cols)
    s_term = jnp.einsum("qrd,cd->qrc", a_all[:, 0], w_all[0], preferred_element_type=jnp.float32)
    c_term = jnp.einsum("qrd,cd->qrc", a_all[:, 1], w_all[1], preferred_element_type=jnp.float32)
    term = (gate[:, None, :] * s_term + c_term).astype(jnp.bfloat16)
    term = term.reshape(quads, rows, parts, group // parts, cols).transpose(0, 2, 1, 3, 4)
    term = term.reshape(quads * parts, rows, group // parts, cols)
    got = lax.all_to_all(term, ("q", "tp"), 0, 0, tiled=True)
    got = got.reshape(quads, parts, rows, group // parts, cols).astype(jnp.float32)
    total = jnp.sum(got, axis=1)
    total = total.transpose(1, 2, 0, 3).reshape(rows, (group // parts) * quads * cols)
    branch = total.astype(jnp.bfloat16).astype(jnp.float32)

    base = slot * tiles
    row_pos = jnp.concatenate(
        [base + jnp.arange(tiles, dtype=jnp.int32), jnp.stack([base - 1, base + tiles])]
    )
    row_valid = (row_pos >= 0) & (row_pos < my_len) & (row_pos < group * tiles)
    branch = jnp.where(row_valid[:, None], branch, 0.0)
    own = branch[:tiles]
    prev_rows = jnp.concatenate([branch[tiles : tiles + 1], own[:-1]], axis=0)
    next_rows = jnp.concatenate([own[1:], branch[tiles + 1 : tiles + 2]], axis=0)
    vel = own + mix_coef[None, :] * (prev_rows + next_rows - 2.0 * own)
    vel = jnp.where(row_valid[:tiles, None], vel, 0.0)
    frac = 1.0 - my_step.astype(jnp.float32) / STEPS
    sigma = 5.0 * frac / (1.0 + 4.0 * frac)
    updated = latent.astype(jnp.float32) + sigma * vel
    return (vel.astype(jnp.bfloat16), updated)


def solution(mesh):
    req = mesh.shape["req"]
    devices = mesh.devices.reshape(req // TENANTS, TENANTS, mesh.shape["tp"])
    split = Mesh(devices, ("z", "q", "tp"))
    rows = ("z", "q")
    placed = (
        P(rows, "tp"),
        P(rows, "tp"),
        P(rows, "tp"),
        P(rows, "tp"),
        P(rows, "tp"),
        P(rows, "tp"),
        P("tp", rows),
        P("tp", rows),
        P(),
        P("tp"),
        P(rows, "tp"),
        P(),
        P(),
        P(),
    )
    return jax.shard_map(
        shards,
        mesh=split,
        in_specs=placed,
        out_specs=(P(rows, "tp"), P(rows, "tp")),
        check_vma=False,
    )
```

```python
import jax
import jax.numpy as jnp
from jax import lax
from jax.experimental import pallas as pl
from jax.experimental.pallas import tpu as pltpu
from jax.sharding import Mesh, PartitionSpec as P

DH = 128
TENANTS = 4
STEPS = 50


def attention_pair(lens, query, cross_query, blocks, *, tiles, text_rows, cols):
    group = len(blocks)
    feat = query.shape[1]
    rows = tiles + 16
    heads = feat // DH
    scale = 1.0 / DH**0.5
    t_at = 2 * tiles
    w_at = t_at + 2 * text_rows
    edge_at = w_at + 2 * cols

    def attend_all(q_ref, k_ref, v_ref, ok, o_ref, which):
        for h in range(heads):
            lanes = pl.ds(h * DH, DH)
            s = lax.dot_general(
                q_ref[:, lanes], k_ref[:, lanes], (((1,), (1,)), ((), ())), preferred_element_type=jnp.float32
            )
            s = jnp.where(ok, s * scale, -1e30)
            m = s.max(axis=-1, keepdims=True)
            p = jnp.where(ok, jnp.exp(s - m), 0.0)
            den = jnp.sum(p, axis=-1, keepdims=True)
            acc = jnp.dot(p.astype(jnp.bfloat16), v_ref[:, lanes], preferred_element_type=jnp.float32)
            o_ref[which, :, lanes] = (acc / den)[: tiles + 2].astype(o_ref.dtype)

    def kernel(lens_ref, query_ref, cquery_ref, *refs):
        bufs = refs[:group]
        o_ref, w_ref, tk_ref, tv_ref, k_ref, v_ref, q_ref, cq_ref = refs[group:]
        n_keys = lens_ref[0]
        n_text = lens_ref[1]
        here = lens_ref[2]
        before = bufs[group - 1][pl.ds(edge_at, 16), :].astype(jnp.float32)
        after = bufs[1][pl.ds(edge_at, 16), :].astype(jnp.float32)
        row = lax.broadcasted_iota(jnp.int32, (16, feat), 0)
        q_ref[pl.ds(0, tiles), :] = query_ref[...]
        cq_ref[pl.ds(0, tiles), :] = cquery_ref[...]
        q_tail = jnp.where(row == 0, before[1:2], jnp.where(row == 1, after[0:1], 0.0))
        cq_tail = jnp.where(row == 0, before[3:4], jnp.where(row == 1, after[2:3], 0.0))
        q_ref[pl.ds(tiles, 16), :] = q_tail.astype(q_ref.dtype)
        cq_ref[pl.ds(tiles, 16), :] = cq_tail.astype(cq_ref.dtype)

        self_valid = lax.broadcasted_iota(jnp.int32, (1, group * tiles), 1) < n_keys
        text_valid = lax.broadcasted_iota(jnp.int32, (1, group * text_rows), 1) < n_text

        for j in range(group):
            at = (here + j) % group
            buf = bufs[j]
            tk_ref[pl.ds(pl.multiple_of(at * text_rows, 16), text_rows), :] = buf[pl.ds(t_at, text_rows), :]
            tv_ref[pl.ds(pl.multiple_of(at * text_rows, 16), text_rows), :] = buf[
                pl.ds(t_at + text_rows, text_rows), :
            ]
            k_ref[pl.ds(pl.multiple_of(at * tiles, 16), tiles), :] = buf[pl.ds(0, tiles), :]
            v_ref[pl.ds(pl.multiple_of(at * tiles, 16), tiles), :] = buf[pl.ds(tiles, tiles), :]
            w_ref[0, pl.ds(pl.multiple_of(at * cols, 16), cols), :] = buf[pl.ds(w_at, cols), :]
            w_ref[1, pl.ds(pl.multiple_of(at * cols, 16), cols), :] = buf[pl.ds(w_at + cols, cols), :]
        attend_all(q_ref, k_ref, v_ref, self_valid, o_ref, 0)
        attend_all(cq_ref, tk_ref, tv_ref, text_valid, o_ref, 1)

    vmem = pltpu.MemorySpace.VMEM
    dtype = query.dtype
    return pl.pallas_call(
        kernel,
        out_shape=(
            jax.ShapeDtypeStruct((2, tiles + 2, feat), dtype),
            jax.ShapeDtypeStruct((2, group * cols, feat), dtype),
        ),
        in_specs=[pl.BlockSpec(memory_space=pltpu.MemorySpace.SMEM)]
        + [pl.BlockSpec(memory_space=vmem)] * (2 + group),
        out_specs=(pl.BlockSpec(memory_space=vmem), pl.BlockSpec(memory_space=vmem)),
        scratch_shapes=[pltpu.VMEM((group * text_rows, feat), dtype)] * 2
        + [pltpu.VMEM((group * tiles, feat), dtype)] * 2
        + [pltpu.VMEM((rows, feat), dtype)] * 2,
    )(lens, query, cross_query, *blocks)


def pack_block(key, value, text_key, text_value, w_self_t, w_cross_t, query, cross_query):
    pieces = (key, value, text_key, text_value, w_self_t, w_cross_t)
    starts = [0]
    for piece in pieces:
        starts.append(starts[-1] + piece.shape[0])
    edge_rows = 16
    feat = key.shape[1]
    last = query.shape[0] - 1

    def kernel(k_ref, v_ref, tk_ref, tv_ref, ws_ref, wc_ref, q_ref, cq_ref, o_ref):
        refs = (k_ref, v_ref, tk_ref, tv_ref, ws_ref, wc_ref)
        for ref, at in zip(refs, starts):
            o_ref[pl.ds(at, ref.shape[0]), :] = ref[...]
        q = q_ref[...].astype(jnp.float32)
        cq = cq_ref[...].astype(jnp.float32)
        row = lax.broadcasted_iota(jnp.int32, (edge_rows, feat), 0)
        edges = jnp.where(row == 0, q[0:1], 0.0)
        edges = jnp.where(row == 1, q[last : last + 1], edges)
        edges = jnp.where(row == 2, cq[0:1], edges)
        edges = jnp.where(row == 3, cq[last : last + 1], edges)
        o_ref[pl.ds(starts[-1], edge_rows), :] = edges.astype(o_ref.dtype)

    vmem = pltpu.MemorySpace.VMEM
    return pl.pallas_call(
        kernel,
        out_shape=jax.ShapeDtypeStruct((starts[-1] + edge_rows, feat), key.dtype),
        in_specs=[pl.BlockSpec(memory_space=vmem)] * 8,
        out_specs=pl.BlockSpec(memory_space=vmem),
    )(key, value, text_key, text_value, w_self_t, w_cross_t, query, cross_query)


def shards(
    query,
    key,
    value,
    cross_query,
    text_key,
    text_value,
    wo_self,
    wo_cross,
    attn_gate,
    mix_coef,
    latent,
    tenant_len,
    text_len,
    t_index,
):
    tiles, feat = query.shape
    text_rows = text_key.shape[0]
    cols = wo_self.shape[1]
    group = lax.axis_size("z")
    quads = lax.axis_size("q")
    parts = lax.axis_size("tp")
    slot = lax.axis_index("z")
    tenant = lax.axis_index("q")
    picker = jnp.arange(TENANTS) == tenant
    my_len = jnp.sum(jnp.where(picker, tenant_len, 0))
    my_text = jnp.sum(jnp.where(picker, text_len, 0))
    my_step = jnp.sum(jnp.where(picker, t_index, 0))

    packed = pack_block(key, value, text_key, text_value, wo_self.T, wo_cross.T, query, cross_query)
    ahead = [(i, (i + 1) % group) for i in range(group)]
    behind = [(i, (i - 1) % group) for i in range(group)]
    forward, backward = [packed], [packed]
    for t in range(1, group // 2 + 1):
        forward.append(lax.ppermute(forward[-1], "z", ahead))
        if t < group - group // 2:
            backward.append(lax.ppermute(backward[-1], "z", behind))
    blocks = backward + forward[len(forward) - 1 : 0 : -1]
    lens = jnp.stack([my_len, my_text, slot]).astype(jnp.int32)
    a_pair, w_all = attention_pair(lens, query, cross_query, blocks, tiles=tiles, text_rows=text_rows, cols=cols)

    a_all = lax.all_gather(a_pair, "q", axis=0, tiled=False)
    rows = tiles + 2
    gate = attn_gate.reshape(TENANTS, group, quads, cols)
    gate = lax.dynamic_index_in_dim(gate, tenant, axis=2, keepdims=False).reshape(TENANTS, group * cols)
    s_term = jnp.einsum("qrd,cd->qrc", a_all[:, 0], w_all[0], preferred_element_type=jnp.float32)
    c_term = jnp.einsum("qrd,cd->qrc", a_all[:, 1], w_all[1], preferred_element_type=jnp.float32)
    term = (gate[:, None, :] * s_term + c_term).astype(jnp.bfloat16)
    term = term.reshape(quads, rows, parts, group // parts, cols).transpose(0, 2, 1, 3, 4)
    term = term.reshape(quads * parts, rows, group // parts, cols)
    got = lax.all_to_all(term, ("q", "tp"), 0, 0, tiled=True)
    got = got.reshape(quads, parts, rows, group // parts, cols).astype(jnp.float32)
    total = jnp.sum(got, axis=1)
    total = total.transpose(1, 2, 0, 3).reshape(rows, (group // parts) * quads * cols)
    branch = total.astype(jnp.bfloat16).astype(jnp.float32)

    base = slot * tiles
    row_pos = jnp.concatenate(
        [base + jnp.arange(tiles, dtype=jnp.int32), jnp.stack([base - 1, base + tiles])]
    )
    row_valid = (row_pos >= 0) & (row_pos < my_len) & (row_pos < group * tiles)
    branch = jnp.where(row_valid[:, None], branch, 0.0)
    own = branch[:tiles]
    prev_rows = jnp.concatenate([branch[tiles : tiles + 1], own[:-1]], axis=0)
    next_rows = jnp.concatenate([own[1:], branch[tiles + 1 : tiles + 2]], axis=0)
    vel = own + mix_coef[None, :] * (prev_rows + next_rows - 2.0 * own)
    vel = jnp.where(row_valid[:tiles, None], vel, 0.0)
    frac = 1.0 - my_step.astype(jnp.float32) / STEPS
    sigma = 5.0 * frac / (1.0 + 4.0 * frac)
    updated = latent.astype(jnp.float32) + sigma * vel
    return (vel.astype(jnp.bfloat16), updated)


def solution(mesh):
    req = mesh.shape["req"]
    devices = mesh.devices.reshape(req // TENANTS, TENANTS, mesh.shape["tp"])
    split = Mesh(devices, ("z", "q", "tp"))
    rows = ("z", "q")
    placed = (
        P(rows, "tp"),
        P(rows, "tp"),
        P(rows, "tp"),
        P(rows, "tp"),
        P(rows, "tp"),
        P(rows, "tp"),
        P("tp", rows),
        P("tp", rows),
        P(),
        P("tp"),
        P(rows, "tp"),
        P(),
        P(),
        P(),
    )
    return jax.shard_map(
        shards,
        mesh=split,
        in_specs=placed,
        out_specs=(P(rows, "tp"), P(rows, "tp")),
        check_vma=False,
    )
```

```python
import jax
import jax.numpy as jnp
from jax import lax
from jax.experimental import pallas as pl
from jax.experimental.pallas import tpu as pltpu
from jax.sharding import Mesh, PartitionSpec as P

DH = 128
TENANTS = 4
STEPS = 50


def attention_pair(lens, query, cross_query, blocks, *, tiles, text_rows, cols):
    group = len(blocks)
    feat = query.shape[1]
    rows = tiles + 16
    heads = feat // DH
    scale = 1.0 / DH**0.5
    t_at = 2 * tiles
    w_at = t_at + 2 * text_rows
    edge_at = w_at + 2 * cols

    def attend_all(q_ref, k_ref, v_ref, ok, o_ref, which):
        for h in range(heads):
            lanes = pl.ds(h * DH, DH)
            s = lax.dot_general(
                q_ref[:, lanes], k_ref[:, lanes], (((1,), (1,)), ((), ())), preferred_element_type=jnp.float32
            )
            s = jnp.where(ok, s * scale, -1e30)
            m = s.max(axis=-1, keepdims=True)
            p = jnp.where(ok, jnp.exp(s - m), 0.0)
            den = jnp.sum(p, axis=-1, keepdims=True)
            acc = jnp.dot(p.astype(jnp.bfloat16), v_ref[:, lanes], preferred_element_type=jnp.float32)
            o_ref[which, :, lanes] = (acc / den)[: tiles + 2].astype(o_ref.dtype)

    def kernel(lens_ref, query_ref, cquery_ref, *refs):
        bufs = refs[:group]
        o_ref, w_ref, tk_ref, tv_ref, k_ref, v_ref, q_ref, cq_ref = refs[group:]
        n_keys = lens_ref[0]
        n_text = lens_ref[1]
        here = lens_ref[2]
        before = bufs[group - 1][pl.ds(edge_at, 16), :].astype(jnp.float32)
        after = bufs[1][pl.ds(edge_at, 16), :].astype(jnp.float32)
        row = lax.broadcasted_iota(jnp.int32, (16, feat), 0)
        q_ref[pl.ds(0, tiles), :] = query_ref[...]
        cq_ref[pl.ds(0, tiles), :] = cquery_ref[...]
        q_tail = jnp.where(row == 0, before[1:2], jnp.where(row == 1, after[0:1], 0.0))
        cq_tail = jnp.where(row == 0, before[3:4], jnp.where(row == 1, after[2:3], 0.0))
        q_ref[pl.ds(tiles, 16), :] = q_tail.astype(q_ref.dtype)
        cq_ref[pl.ds(tiles, 16), :] = cq_tail.astype(cq_ref.dtype)

        self_valid = lax.broadcasted_iota(jnp.int32, (1, group * tiles), 1) < n_keys
        text_valid = lax.broadcasted_iota(jnp.int32, (1, group * text_rows), 1) < n_text

        for j in range(group):
            at = (here + j) % group
            buf = bufs[j]
            tk_ref[pl.ds(pl.multiple_of(at * text_rows, 16), text_rows), :] = buf[pl.ds(t_at, text_rows), :]
            tv_ref[pl.ds(pl.multiple_of(at * text_rows, 16), text_rows), :] = buf[
                pl.ds(t_at + text_rows, text_rows), :
            ]
            k_ref[pl.ds(pl.multiple_of(at * tiles, 16), tiles), :] = buf[pl.ds(0, tiles), :]
            v_ref[pl.ds(pl.multiple_of(at * tiles, 16), tiles), :] = buf[pl.ds(tiles, tiles), :]
            w_ref[0, pl.ds(pl.multiple_of(at * cols, 16), cols), :] = buf[pl.ds(w_at, cols), :]
            w_ref[1, pl.ds(pl.multiple_of(at * cols, 16), cols), :] = buf[pl.ds(w_at + cols, cols), :]
        attend_all(q_ref, k_ref, v_ref, self_valid, o_ref, 0)
        attend_all(cq_ref, tk_ref, tv_ref, text_valid, o_ref, 1)

    vmem = pltpu.MemorySpace.VMEM
    dtype = query.dtype
    return pl.pallas_call(
        kernel,
        out_shape=(
            jax.ShapeDtypeStruct((2, tiles + 2, feat), dtype),
            jax.ShapeDtypeStruct((2, group * cols, feat), dtype),
        ),
        in_specs=[pl.BlockSpec(memory_space=pltpu.MemorySpace.SMEM)]
        + [pl.BlockSpec(memory_space=vmem)] * (2 + group),
        out_specs=(pl.BlockSpec(memory_space=vmem), pl.BlockSpec(memory_space=vmem)),
        scratch_shapes=[pltpu.VMEM((group * text_rows, feat), dtype)] * 2
        + [pltpu.VMEM((group * tiles, feat), dtype)] * 2
        + [pltpu.VMEM((rows, feat), dtype)] * 2,
    )(lens, query, cross_query, *blocks)


def pack_block(key, value, text_key, text_value, w_self_t, w_cross_t, query, cross_query):
    pieces = (key, value, text_key, text_value, w_self_t, w_cross_t)
    starts = [0]
    for piece in pieces:
        starts.append(starts[-1] + piece.shape[0])
    edge_rows = 16
    feat = key.shape[1]
    last = query.shape[0] - 1

    def kernel(k_ref, v_ref, tk_ref, tv_ref, ws_ref, wc_ref, q_ref, cq_ref, o_ref, edge_ref, sems):
        refs = (k_ref, v_ref, tk_ref, tv_ref, ws_ref, wc_ref)
        copies = []
        for i, (ref, at) in enumerate(zip(refs, starts)):
            copy = pltpu.make_async_copy(ref, o_ref.at[pl.ds(at, ref.shape[0])], sems.at[i])
            copy.start()
            copies.append(copy)
        q = q_ref[...].astype(jnp.float32)
        cq = cq_ref[...].astype(jnp.float32)
        row = lax.broadcasted_iota(jnp.int32, (edge_rows, feat), 0)
        edges = jnp.where(row == 0, q[0:1], 0.0)
        edges = jnp.where(row == 1, q[last : last + 1], edges)
        edges = jnp.where(row == 2, cq[0:1], edges)
        edges = jnp.where(row == 3, cq[last : last + 1], edges)
        edge_ref[...] = edges.astype(edge_ref.dtype)
        copy = pltpu.make_async_copy(edge_ref, o_ref.at[pl.ds(starts[-1], edge_rows)], sems.at[len(refs)])
        copy.start()
        copies.append(copy)
        for copy in copies:
            copy.wait()

    vmem = pltpu.MemorySpace.VMEM
    hbm = pl.BlockSpec(memory_space=pl.ANY)
    return pl.pallas_call(
        kernel,
        out_shape=jax.ShapeDtypeStruct((starts[-1] + edge_rows, feat), key.dtype),
        in_specs=[hbm] * 6 + [pl.BlockSpec(memory_space=vmem)] * 2,
        out_specs=hbm,
        scratch_shapes=[pltpu.VMEM((edge_rows, feat), key.dtype), pltpu.SemaphoreType.DMA((len(pieces) + 1,))],
    )(key, value, text_key, text_value, w_self_t, w_cross_t, query, cross_query)


def shards(
    query,
    key,
    value,
    cross_query,
    text_key,
    text_value,
    wo_self,
    wo_cross,
    attn_gate,
    mix_coef,
    latent,
    tenant_len,
    text_len,
    t_index,
):
    tiles, feat = query.shape
    text_rows = text_key.shape[0]
    cols = wo_self.shape[1]
    group = lax.axis_size("z")
    quads = lax.axis_size("q")
    parts = lax.axis_size("tp")
    slot = lax.axis_index("z")
    tenant = lax.axis_index("q")
    picker = jnp.arange(TENANTS) == tenant
    my_len = jnp.sum(jnp.where(picker, tenant_len, 0))
    my_text = jnp.sum(jnp.where(picker, text_len, 0))
    my_step = jnp.sum(jnp.where(picker, t_index, 0))

    packed = pack_block(key, value, text_key, text_value, wo_self.T, wo_cross.T, query, cross_query)
    ahead = [(i, (i + 1) % group) for i in range(group)]
    behind = [(i, (i - 1) % group) for i in range(group)]
    forward, backward = [packed], [packed]
    for t in range(1, group // 2 + 1):
        forward.append(lax.ppermute(forward[-1], "z", ahead))
        if t < group - group // 2:
            backward.append(lax.ppermute(backward[-1], "z", behind))
    blocks = backward + forward[len(forward) - 1 : 0 : -1]
    lens = jnp.stack([my_len, my_text, slot]).astype(jnp.int32)
    a_pair, w_all = attention_pair(lens, query, cross_query, blocks, tiles=tiles, text_rows=text_rows, cols=cols)

    a_all = lax.all_gather(a_pair, "q", axis=0, tiled=False)
    rows = tiles + 2
    gate = attn_gate.reshape(TENANTS, group, quads, cols)
    gate = lax.dynamic_index_in_dim(gate, tenant, axis=2, keepdims=False).reshape(TENANTS, group * cols)
    s_term = jnp.einsum("qrd,cd->qrc", a_all[:, 0], w_all[0], preferred_element_type=jnp.float32)
    c_term = jnp.einsum("qrd,cd->qrc", a_all[:, 1], w_all[1], preferred_element_type=jnp.float32)
    term = (gate[:, None, :] * s_term + c_term).astype(jnp.bfloat16)
    term = term.reshape(quads, rows, parts, group // parts, cols).transpose(0, 2, 1, 3, 4)
    term = term.reshape(quads * parts, rows, group // parts, cols)
    got = lax.all_to_all(term, ("q", "tp"), 0, 0, tiled=True)
    got = got.reshape(quads, parts, rows, group // parts, cols).astype(jnp.float32)
    total = jnp.sum(got, axis=1)
    total = total.transpose(1, 2, 0, 3).reshape(rows, (group // parts) * quads * cols)
    branch = total.astype(jnp.bfloat16).astype(jnp.float32)

    base = slot * tiles
    row_pos = jnp.concatenate(
        [base + jnp.arange(tiles, dtype=jnp.int32), jnp.stack([base - 1, base + tiles])]
    )
    row_valid = (row_pos >= 0) & (row_pos < my_len) & (row_pos < group * tiles)
    branch = jnp.where(row_valid[:, None], branch, 0.0)
    own = branch[:tiles]
    prev_rows = jnp.concatenate([branch[tiles : tiles + 1], own[:-1]], axis=0)
    next_rows = jnp.concatenate([own[1:], branch[tiles + 1 : tiles + 2]], axis=0)
    vel = own + mix_coef[None, :] * (prev_rows + next_rows - 2.0 * own)
    vel = jnp.where(row_valid[:tiles, None], vel, 0.0)
    frac = 1.0 - my_step.astype(jnp.float32) / STEPS
    sigma = 5.0 * frac / (1.0 + 4.0 * frac)
    updated = latent.astype(jnp.float32) + sigma * vel
    return (vel.astype(jnp.bfloat16), updated)


def solution(mesh):
    req = mesh.shape["req"]
    devices = mesh.devices.reshape(req // TENANTS, TENANTS, mesh.shape["tp"])
    split = Mesh(devices, ("z", "q", "tp"))
    rows = ("z", "q")
    placed = (
        P(rows, "tp"),
        P(rows, "tp"),
        P(rows, "tp"),
        P(rows, "tp"),
        P(rows, "tp"),
        P(rows, "tp"),
        P("tp", rows),
        P("tp", rows),
        P(),
        P("tp"),
        P(rows, "tp"),
        P(),
        P(),
        P(),
    )
    return jax.shard_map(
        shards,
        mesh=split,
        in_specs=placed,
        out_specs=(P(rows, "tp"), P(rows, "tp")),
        check_vma=False,
    )
```
